32 devices in a mesh: img: 8 (over z, core), slab: 4 (over y, x).
Axes of the slice: x: 2, y: 2, z: 4, core: 2. Of those that a mesh axis runs over, the one named last changes fastest.
Arguments:
- image_masses: float32 [8, 3072, 3072], P('img', 'slab'), may hold values from 0.1 to 10
- dual_multipliers: float32 [8, 3072, 3072], P('img', 'slab'), may hold values from 0.1 to 10
- fraction_tops: int32 [8], P('img'), may hold values from 1 to 8
- banded_submatrices: bfloat16 [24, 3, 128, 128], replicated, as said below
- band_starts: int32 [24, 3], replicated, may hold values from -2 to 2, as said below
Outputs:
- barycenter: float32 [3072, 3072], P('slab')
- new_scalings: float32 [8, 3072, 3072], P('img', 'slab')
The draws below stay inside these ranges and needn't reach their ends.
Inputs may be any that keep to these rules, and one draw needn't show every extreme that they name: `band_starts`: each row of offsets holds three consecutive numbers in increasing order; the first row is 0, 1, 2 and the last row is -2, -1, 0. `banded_submatrices`: all entries are positive.
All inputs are finite; a program needn't handle non-finite values.
Results may differ from the reference program's by a relative error of at most 0.0032.
Values may be sent and summed in bfloat16 or wider, within the bound.
No kernel may reach another device: no remote copies, remote signals or barrier semaphores. Data moves between devices by JAX's collectives and lax.ppermute only.
A program may use at most 192 MiB of HBM per device.

```python
import jax
import jax.numpy as jnp
from jax import lax

LATTICE_EXTENT = 3072
BLOCK = 128
ITERS = 2
NBLOCKS = 24
PICTURE_TOTAL = 8
ROWS_DEV = 768


def block_shifts(key):
    shift = jax.random.randint(jax.random.fold_in(key, 11), (NBLOCKS,), -1, 2)
    shift = shift.at[0].set(1).at[NBLOCKS - 1].set(-1)
    return shift[:, None] + jnp.arange(3, dtype=jnp.int32)[None, :] - 1


def draw_band_starts(key, part):
    return block_shifts(key).astype(jnp.int32)


def draw_banded_submatrices(key, part):
    shifts = block_shifts(key)
    centre = (shifts == 0).astype(jnp.float32)
    offsets = shifts.astype(jnp.float32)
    remaining_key, key_diag = jax.random.split(jax.random.fold_in(key, 23))
    shape = (NBLOCKS, 3, BLOCK, BLOCK)
    spread = jax.random.uniform(remaining_key, shape, jnp.float32, -1.15, 1.15)
    row_place = jnp.arange(BLOCK, dtype=jnp.float32)[:, None]
    col_place = jnp.arange(BLOCK, dtype=jnp.float32)[None, :]
    distance = offsets[:, :, None, None] * BLOCK + col_place[None, None] - row_place[None, None]
    reach_pixels = BLOCK / 4.0
    profile = 0.15 + 1.5 * jnp.exp(-0.5 * (distance / reach_pixels) * (distance / reach_pixels))
    off_diagonal = profile * jnp.exp(spread) * (0.35 / BLOCK)
    diag_scale = 0.5 * jnp.exp(jax.random.uniform(key_diag, (NBLOCKS, 3, BLOCK), jnp.float32, -0.5, 0.5))
    identity = jnp.eye(BLOCK, dtype=jnp.float32)
    full = off_diagonal + centre[:, :, None, None] * diag_scale[:, :, :, None] * identity
    return full.astype(jnp.bfloat16)


def pattern(key, level_low, level_high, row_coeff, col_coeff, rough_coeff):
    slab_count = LATTICE_EXTENT // ROWS_DEV
    key_flip, key_level, key_rows, key_cols, key_rough = jax.random.split(key, 5)
    flipped = jax.random.randint(key_flip, (PICTURE_TOTAL, 1), 0, 2)
    slab_index = jnp.arange(slab_count, dtype=jnp.int32)[None, :]
    parity = ((slab_index + flipped) % 2).astype(jnp.float32)
    levels = (1.0 - 2.0 * parity) * jax.random.uniform(key_level, (PICTURE_TOTAL, slab_count), jnp.float32, level_low, level_high)
    positions = jnp.arange(LATTICE_EXTENT, dtype=jnp.int32)
    level_rows = jnp.take(levels, positions // ROWS_DEV, axis=1)
    sawtooth = ((positions % BLOCK).astype(jnp.float32) + 0.5) / BLOCK - 0.5
    row_sign = (2 * jax.random.randint(key_rows, (PICTURE_TOTAL,), 0, 2) - 1).astype(jnp.float32)
    col_sign = (2 * jax.random.randint(key_cols, (PICTURE_TOTAL,), 0, 2) - 1).astype(jnp.float32)
    roughness = jax.random.uniform(key_rough, (PICTURE_TOTAL, LATTICE_EXTENT, LATTICE_EXTENT), jnp.float32, -rough_coeff, rough_coeff)
    exponent = level_rows[:, :, None] + (row_coeff * row_sign)[:, None, None] * sawtooth[None, :, None]
    exponent = exponent + (col_coeff * col_sign)[:, None, None] * sawtooth[None, None, :] + roughness
    return jnp.exp(exponent)


def draw_dual_multipliers(key, part):
    inner_key = jax.random.fold_in(key, 31)
    return pattern(inner_key, 0.3, 0.5, 1.8, 0.4, 0.35)


def draw_image_masses(key, part):
    inner_key = jax.random.fold_in(key, 37)
    return pattern(inner_key, 0.3, 0.55, 2.0, 0.4, 0.45)


def place_ends(values, rng, least, top_value):
    dims = values.shape
    place = [jax.random.randint(jax.random.fold_in(rng, axis), (), 0, dims[axis]) for axis in range(len(dims))]
    values = values.at[tuple(place)].set(least)
    longest = dims.index(max(dims))
    place[longest] = (place[longest] + 1) % dims[longest]
    return values.at[tuple(place)].set(top_value)


def setup_inputs(seed: int = 0) -> dict:
    seeds = jax.random.split(jax.random.key(seed), 6)
    image_masses = draw_image_masses(jax.random.fold_in(seeds[5], 71), 0)
    dual_multipliers = draw_dual_multipliers(jax.random.fold_in(seeds[5], 71), 0)
    fraction_tops = place_ends(jax.random.randint(seeds[2], (PICTURE_TOTAL,), 1, 9), jax.random.fold_in(seeds[2], 1), 1, 8).astype(jnp.int32)
    banded_submatrices = draw_banded_submatrices(jax.random.fold_in(seeds[5], 71), 0)
    band_starts = draw_band_starts(jax.random.fold_in(seeds[5], 71), 0)
    return dict(image_masses=image_masses, dual_multipliers=dual_multipliers, fraction_tops=fraction_tops, banded_submatrices=banded_submatrices, band_starts=band_starts)


def column_sweep(field, banded_submatrices, band_starts):
    block_stack = banded_submatrices.shape[0]
    width = banded_submatrices.shape[2]
    lead = field.shape[:-1]
    split = field.reshape(lead + (block_stack, width))
    padded = jnp.pad(split, ((0, 0), (2, 2), (0, 0)))
    block_index = (jnp.arange(block_stack, dtype=jnp.int32)[:, None] + band_starts + 2).astype(jnp.int32)
    gathered = jnp.take(padded, block_index, axis=1)
    result = jnp.einsum("rbjk,bjik->rbi", gathered.astype(jnp.float32), banded_submatrices.astype(jnp.float32))
    return result.reshape(lead + (block_stack * width,))


def rows_pass(padded, banded_submatrices, band_starts):
    block_stack = banded_submatrices.shape[0]
    width = banded_submatrices.shape[2]
    columns = padded.shape[-1]
    split = padded.reshape((block_stack + 4, width, columns))
    block_index = (jnp.arange(block_stack, dtype=jnp.int32)[:, None] + band_starts + 2).astype(jnp.int32)
    gathered = jnp.take(split, block_index, axis=0)
    result = jnp.einsum("bjkc,bjik->bic", gathered.astype(jnp.float32), banded_submatrices.astype(jnp.float32))
    return result.reshape((block_stack * width, columns))


def apply_kernel(field, banded_submatrices, band_starts):
    inner = column_sweep(field, banded_submatrices, band_starts).astype(jnp.bfloat16)
    width = banded_submatrices.shape[2]
    padded = jnp.pad(inner, ((2 * width, 2 * width), (0, 0)))
    return rows_pass(padded, banded_submatrices, band_starts).astype(jnp.bfloat16)


def reference(image_masses, dual_multipliers, fraction_tops, banded_submatrices, band_starts):
    total_weight = jnp.sum(fraction_tops).astype(jnp.float32)
    weights = fraction_tops.astype(jnp.float32)
    latest_multiplier = dual_multipliers
    barycenter = jnp.zeros((LATTICE_EXTENT, LATTICE_EXTENT), jnp.float32)

    def one_image(pair):
        density, scaling = pair
        kernel_v = apply_kernel(scaling.astype(jnp.bfloat16), banded_submatrices, band_starts)
        scaled_u = (density / kernel_v.astype(jnp.float32)).astype(jnp.bfloat16)
        return apply_kernel(scaled_u, banded_submatrices, band_starts)

    for iteration in range(ITERS):
        kernel_u = lax.map(one_image, (image_masses, latest_multiplier))
        log_sum = jnp.einsum("i,irc->rc", weights, jnp.log(kernel_u.astype(jnp.float32)))
        barycenter = jnp.exp(log_sum / total_weight)
        latest_multiplier = barycenter[None] / kernel_u.astype(jnp.float32)
    return barycenter, latest_multiplier
```

```python
import jax
import jax.numpy as jnp
from jax import lax
from jax.sharding import PartitionSpec as P

ITERS = 2
HALO_BLOCKS = 2


def dense_blocks(banded_submatrices, band_starts, first_row, rows, first_col, cols):
    width = banded_submatrices.shape[2]
    block_rows = lax.dynamic_slice_in_dim(banded_submatrices, first_row, rows, axis=0)
    starts = lax.dynamic_slice_in_dim(band_starts, first_row, rows, axis=0)
    total_blocks = banded_submatrices.shape[0]
    global_col = first_row + jnp.arange(rows, dtype=jnp.int32)[:, None] + starts
    in_range = (global_col >= 0) & (global_col < total_blocks)
    local_col = global_col - first_col
    matches = (local_col[:, :, None] == jnp.arange(cols, dtype=jnp.int32)[None, None, :]) & in_range[:, :, None]
    picked = jnp.where(matches[:, :, :, None, None], block_rows[:, :, None], jnp.zeros((), jnp.bfloat16))
    blocks = jnp.sum(picked, axis=1)
    return blocks.transpose(0, 2, 1, 3).reshape((rows * width, cols * width))


def per_device(image_masses, dual_multipliers, fraction_tops, banded_submatrices, band_starts, nslab):
    width = banded_submatrices.shape[2]
    total_blocks = banded_submatrices.shape[0]
    rows = image_masses.shape[1]
    local_blocks = rows // width
    halo = HALO_BLOCKS * width
    slab = lax.axis_index("slab")
    first = slab * local_blocks

    a_full = dense_blocks(banded_submatrices, band_starts, 0, total_blocks, 0, total_blocks)
    a_local = dense_blocks(
        banded_submatrices, band_starts, first, local_blocks, first - HALO_BLOCKS, local_blocks + 2 * HALO_BLOCKS
    )
    a_prev = a_local[:, :halo]
    a_mid = a_local[:, halo : halo + rows]
    a_next = a_local[:, halo + rows :]

    total_weight = lax.psum(jnp.sum(fraction_tops).astype(jnp.float32), "img")
    weight = fraction_tops.astype(jnp.float32)[0]

    up = [(i, i + 1) for i in range(nslab - 1)]
    down = [(i + 1, i) for i in range(nslab - 1)]

    def column_pass(field):
        return lax.dot_general(
            field, a_full, (((1,), (1,)), ((), ())), preferred_element_type=jnp.float32
        ).astype(jnp.bfloat16)

    def row_pass(inner):
        from_prev = lax.ppermute(inner[rows - halo :], "slab", up)
        from_next = lax.ppermute(inner[:halo], "slab", down)
        total = jnp.dot(a_mid, inner, preferred_element_type=jnp.float32)
        total = total + jnp.dot(a_prev, from_prev, preferred_element_type=jnp.float32)
        total = total + jnp.dot(a_next, from_next, preferred_element_type=jnp.float32)
        return total.astype(jnp.bfloat16)

    def apply_kernel(field):
        return row_pass(column_pass(field))

    masses = image_masses[0]
    scaling = dual_multipliers[0]
    barycenter = None
    for iteration in range(ITERS):
        kernel_v = apply_kernel(scaling.astype(jnp.bfloat16))
        scaled_u = (masses / kernel_v.astype(jnp.float32)).astype(jnp.bfloat16)
        kernel_u = apply_kernel(scaled_u).astype(jnp.float32)
        value_portion = weight * jnp.log(kernel_u)
        barycenter = jnp.exp(lax.psum(value_portion, "img") / total_weight)
        scaling = barycenter / kernel_u
    return (barycenter, scaling[None])


def solution(mesh):
    nslab = mesh.shape["slab"]
    placed = (P("img", "slab", None), P("img", "slab", None), P("img"), P(), P())

    def body(*args):
        return per_device(*args, nslab=nslab)

    return jax.shard_map(
        body,
        mesh=mesh,
        in_specs=placed,
        out_specs=(P("slab", None), P("img", "slab", None)),
        check_vma=False,
    )
```

```python
import jax
import jax.numpy as jnp
from jax import lax
from jax.experimental import pallas as pl
from jax.sharding import PartitionSpec as P

ITERS = 2
HALO = 2
OFFSETS = 2 * HALO + 1


def offset_terms(banded_submatrices, band_starts):
    offsets = jnp.arange(-HALO, HALO + 1, dtype=jnp.int32)
    matches = band_starts[:, None, :] == offsets[None, :, None]
    picked = jnp.where(matches[:, :, :, None, None], banded_submatrices[:, None], jnp.zeros((), jnp.bfloat16))
    return jnp.sum(picked, axis=2)


def column_kernel(x_ref, t_ref, o_ref):
    nblocks = t_ref.shape[0]
    width = t_ref.shape[2]
    x = x_ref[...].astype(jnp.bfloat16)
    for b in range(nblocks):
        acc = None
        for o in range(OFFSETS):
            c = b + o - HALO
            if c < 0 or c >= nblocks:
                continue
            prod = lax.dot_general(
                x[:, c * width : (c + 1) * width],
                t_ref[b, o],
                (((1,), (1,)), ((), ())),
                preferred_element_type=jnp.float32,
            )
            acc = prod if acc is None else acc + prod
        o_ref[:, b * width : (b + 1) * width] = acc.astype(o_ref.dtype)


def column_pass(field, terms, tile_rows=256):
    rows, cols = field.shape
    return pl.pallas_call(
        column_kernel,
        grid=(rows // tile_rows,),
        in_specs=[
            pl.BlockSpec((tile_rows, cols), lambda r: (r, 0)),
            pl.BlockSpec(terms.shape, lambda r: (0, 0, 0, 0)),
        ],
        out_specs=pl.BlockSpec((tile_rows, cols), lambda r: (r, 0)),
        out_shape=jax.ShapeDtypeStruct((rows, cols), jnp.bfloat16),
    )(field, terms)


def row_kernel(prev_ref, mid_ref, next_ref, t_ref, o_ref):
    nlocal = t_ref.shape[0]
    width = t_ref.shape[2]
    for b in range(nlocal):
        acc = None
        for o in range(OFFSETS):
            e = b + o - HALO
            if e < 0:
                src = prev_ref[(e + HALO) * width : (e + HALO + 1) * width, :]
            elif e >= nlocal:
                src = next_ref[(e - nlocal) * width : (e - nlocal + 1) * width, :]
            else:
                src = mid_ref[e * width : (e + 1) * width, :]
            prod = jnp.dot(t_ref[b, o], src, preferred_element_type=jnp.float32)
            acc = prod if acc is None else acc + prod
        o_ref[b * width : (b + 1) * width, :] = acc.astype(o_ref.dtype)


def row_pass(prev, mid, nxt, terms_local, tile_cols=768):
    rows, cols = mid.shape
    halo_rows = prev.shape[0]
    return pl.pallas_call(
        row_kernel,
        grid=(cols // tile_cols,),
        in_specs=[
            pl.BlockSpec((halo_rows, tile_cols), lambda c: (0, c)),
            pl.BlockSpec((rows, tile_cols), lambda c: (0, c)),
            pl.BlockSpec((halo_rows, tile_cols), lambda c: (0, c)),
            pl.BlockSpec(terms_local.shape, lambda c: (0, 0, 0, 0)),
        ],
        out_specs=pl.BlockSpec((rows, tile_cols), lambda c: (0, c)),
        out_shape=jax.ShapeDtypeStruct((rows, cols), jnp.bfloat16),
    )(prev, mid, nxt, terms_local)


def per_device(image_masses, dual_multipliers, fraction_tops, banded_submatrices, band_starts, nslab):
    width = banded_submatrices.shape[2]
    rows = image_masses.shape[1]
    local_blocks = rows // width
    halo = HALO * width
    slab = lax.axis_index("slab")

    terms = offset_terms(banded_submatrices, band_starts)
    terms_local = lax.dynamic_slice_in_dim(terms, slab * local_blocks, local_blocks, axis=0)

    total_weight = lax.psum(jnp.sum(fraction_tops).astype(jnp.float32), "img")
    weight = fraction_tops.astype(jnp.float32)[0]

    up = [(i, i + 1) for i in range(nslab - 1)]
    down = [(i + 1, i) for i in range(nslab - 1)]

    def apply_kernel(field):
        inner = column_pass(field, terms)
        from_prev = lax.ppermute(inner[rows - halo :], "slab", up)
        from_next = lax.ppermute(inner[:halo], "slab", down)
        return row_pass(from_prev, inner, from_next, terms_local)

    masses = image_masses[0]
    scaling = dual_multipliers[0]
    barycenter = None
    for iteration in range(ITERS):
        kernel_v = apply_kernel(scaling.astype(jnp.bfloat16))
        scaled_u = (masses / kernel_v.astype(jnp.float32)).astype(jnp.bfloat16)
        kernel_u = apply_kernel(scaled_u).astype(jnp.float32)
        value_portion = weight * jnp.log(kernel_u)
        barycenter = jnp.exp(lax.psum(value_portion, "img") / total_weight)
        scaling = barycenter / kernel_u
    return (barycenter, scaling[None])


def solution(mesh):
    nslab = mesh.shape["slab"]
    placed = (P("img", "slab", None), P("img", "slab", None), P("img"), P(), P())

    def body(*args):
        return per_device(*args, nslab=nslab)

    return jax.shard_map(
        body,
        mesh=mesh,
        in_specs=placed,
        out_specs=(P("slab", None), P("img", "slab", None)),
        check_vma=False,
    )
```

```python
import jax
import jax.numpy as jnp
from jax import lax
from jax.experimental import pallas as pl
from jax.sharding import PartitionSpec as P

ITERS = 2
HALO = 2
OFFSETS = 2 * HALO + 1


def offset_terms(banded_submatrices, band_starts):
    offsets = jnp.arange(-HALO, HALO + 1, dtype=jnp.int32)
    matches = band_starts[:, None, :] == offsets[None, :, None]
    picked = jnp.where(matches[:, :, :, None, None], banded_submatrices[:, None], jnp.zeros((), jnp.bfloat16))
    return jnp.sum(picked, axis=2)


def column_kernel(x_ref, t_ref, o_ref):
    nblocks = t_ref.shape[0]
    width = t_ref.shape[2]
    x = x_ref[...].astype(jnp.bfloat16)
    for b in range(nblocks):
        acc = None
        for o in range(OFFSETS):
            c = b + o - HALO
            if c < 0 or c >= nblocks:
                continue
            prod = lax.dot_general(
                x[:, c * width : (c + 1) * width],
                t_ref[b, o],
                (((1,), (1,)), ((), ())),
                preferred_element_type=jnp.float32,
            )
            acc = prod if acc is None else acc + prod
        o_ref[:, b * width : (b + 1) * width] = acc.astype(o_ref.dtype)


def column_pass(field, terms, tile_rows=256):
    rows, cols = field.shape
    return pl.pallas_call(
        column_kernel,
        grid=(rows // tile_rows,),
        in_specs=[
            pl.BlockSpec((tile_rows, cols), lambda r: (r, 0)),
            pl.BlockSpec(terms.shape, lambda r: (0, 0, 0, 0)),
        ],
        out_specs=pl.BlockSpec((tile_rows, cols), lambda r: (r, 0)),
        out_shape=jax.ShapeDtypeStruct((rows, cols), jnp.bfloat16),
    )(field, terms)


def row_kernel(prev_ref, mid_ref, next_ref, t_ref, o_ref):
    nlocal = t_ref.shape[0]
    width = t_ref.shape[2]
    for b in range(nlocal):
        acc = None
        for o in range(OFFSETS):
            e = b + o - HALO
            if e < 0:
                src = prev_ref[(e + HALO) * width : (e + HALO + 1) * width, :]
            elif e >= nlocal:
                src = next_ref[(e - nlocal) * width : (e - nlocal + 1) * width, :]
            else:
                src = mid_ref[e * width : (e + 1) * width, :]
            prod = jnp.dot(t_ref[b, o], src, preferred_element_type=jnp.float32)
            acc = prod if acc is None else acc + prod
        o_ref[b * width : (b + 1) * width, :] = acc.astype(o_ref.dtype)


def row_pass(prev, mid, nxt, terms_local, tile_cols=768):
    rows, cols = mid.shape
    halo_rows = prev.shape[0]
    return pl.pallas_call(
        row_kernel,
        grid=(cols // tile_cols,),
        in_specs=[
            pl.BlockSpec((halo_rows, tile_cols), lambda c: (0, c)),
            pl.BlockSpec((rows, tile_cols), lambda c: (0, c)),
            pl.BlockSpec((halo_rows, tile_cols), lambda c: (0, c)),
            pl.BlockSpec(terms_local.shape, lambda c: (0, 0, 0, 0)),
        ],
        out_specs=pl.BlockSpec((rows, tile_cols), lambda c: (0, c)),
        out_shape=jax.ShapeDtypeStruct((rows, cols), jnp.bfloat16),
    )(prev, mid, nxt, terms_local)


def per_device(image_masses, dual_multipliers, fraction_tops, banded_submatrices, band_starts, nslab):
    width = banded_submatrices.shape[2]
    rows = image_masses.shape[1]
    local_blocks = rows // width
    halo = HALO * width
    slab = lax.axis_index("slab")

    terms = offset_terms(banded_submatrices, band_starts)
    terms_local = lax.dynamic_slice_in_dim(terms, slab * local_blocks, local_blocks, axis=0)

    total_weight = lax.psum(jnp.sum(fraction_tops).astype(jnp.float32), "img")
    weight = fraction_tops.astype(jnp.float32)[0]

    up = [(i, i + 1) for i in range(nslab - 1)]
    down = [(i + 1, i) for i in range(nslab - 1)]

    def apply_kernel(field):
        inner = column_pass(field, terms)
        from_prev = lax.ppermute(inner[rows - halo :], "slab", up)
        from_next = lax.ppermute(inner[:halo], "slab", down)
        return row_pass(from_prev, inner, from_next, terms_local)

    masses = image_masses[0]
    scaling = dual_multipliers[0]
    barycenter = None
    for iteration in range(ITERS):
        kernel_v = apply_kernel(scaling.astype(jnp.bfloat16))
        scaled_u = (masses / kernel_v.astype(jnp.float32)).astype(jnp.bfloat16)
        kernel_u = apply_kernel(scaled_u).astype(jnp.float32)
        value_portion = weight * jnp.log(kernel_u)
        if iteration + 1 < ITERS:
            log_sum = lax.psum_scatter(value_portion, "img", scatter_dimension=0, tiled=True)
            barycenter = jnp.exp(log_sum / total_weight).astype(jnp.bfloat16)
            barycenter = lax.all_gather(barycenter, "img", axis=0, tiled=True).astype(jnp.float32)
        else:
            barycenter = jnp.exp(lax.psum(value_portion, "img") / total_weight)
        scaling = barycenter / kernel_u
    return (barycenter, scaling[None])


def solution(mesh):
    nslab = mesh.shape["slab"]
    placed = (P("img", "slab", None), P("img", "slab", None), P("img"), P(), P())

    def body(*args):
        return per_device(*args, nslab=nslab)

    return jax.shard_map(
        body,
        mesh=mesh,
        in_specs=placed,
        out_specs=(P("slab", None), P("img", "slab", None)),
        check_vma=False,
    )
```

```python
import jax
import jax.numpy as jnp
from jax import lax
from jax.experimental import pallas as pl
from jax.sharding import PartitionSpec as P

ITERS = 2
HALO = 2
OFFSETS = 2 * HALO + 1


def offset_terms(banded_submatrices, band_starts):
    offsets = jnp.arange(-HALO, HALO + 1, dtype=jnp.int32)
    matches = band_starts[:, None, :] == offsets[None, :, None]
    picked = jnp.where(matches[:, :, :, None, None], banded_submatrices[:, None], jnp.zeros((), jnp.bfloat16))
    return jnp.sum(picked, axis=2)


def column_kernel(x_ref, t_ref, o_ref):
    nblocks = t_ref.shape[0]
    width = t_ref.shape[2]
    x = x_ref[...].astype(jnp.bfloat16)
    for b in range(nblocks):
        acc = None
        for o in range(OFFSETS):
            c = b + o - HALO
            if c < 0 or c >= nblocks:
                continue
            prod = lax.dot_general(
                x[:, c * width : (c + 1) * width],
                t_ref[b, o],
                (((1,), (1,)), ((), ())),
                preferred_element_type=jnp.float32,
            )
            acc = prod if acc is None else acc + prod
        o_ref[:, b * width : (b + 1) * width] = acc.astype(o_ref.dtype)


def column_pass(field, terms, tile_rows=256):
    rows, cols = field.shape
    return pl.pallas_call(
        column_kernel,
        grid=(rows // tile_rows,),
        in_specs=[
            pl.BlockSpec((tile_rows, cols), lambda r: (r, 0)),
            pl.BlockSpec(terms.shape, lambda r: (0, 0, 0, 0)),
        ],
        out_specs=pl.BlockSpec((tile_rows, cols), lambda r: (r, 0)),
        out_shape=jax.ShapeDtypeStruct((rows, cols), jnp.bfloat16),
    )(field, terms)


def row_kernel(prev_ref, mid_ref, next_ref, t_ref, o_ref):
    nlocal = t_ref.shape[0]
    width = t_ref.shape[2]
    for b in range(nlocal):
        acc = None
        for o in range(OFFSETS):
            e = b + o - HALO
            if e < 0:
                src = prev_ref[(e + HALO) * width : (e + HALO + 1) * width, :]
            elif e >= nlocal:
                src = next_ref[(e - nlocal) * width : (e - nlocal + 1) * width, :]
            else:
                src = mid_ref[e * width : (e + 1) * width, :]
            prod = jnp.dot(t_ref[b, o], src, preferred_element_type=jnp.float32)
            acc = prod if acc is None else acc + prod
        o_ref[b * width : (b + 1) * width, :] = acc.astype(o_ref.dtype)


def row_pass(prev, mid, nxt, terms_local, tile_cols=768):
    rows, cols = mid.shape
    halo_rows = prev.shape[0]
    return pl.pallas_call(
        row_kernel,
        grid=(cols // tile_cols,),
        in_specs=[
            pl.BlockSpec((halo_rows, tile_cols), lambda c: (0, c)),
            pl.BlockSpec((rows, tile_cols), lambda c: (0, c)),
            pl.BlockSpec((halo_rows, tile_cols), lambda c: (0, c)),
            pl.BlockSpec(terms_local.shape, lambda c: (0, 0, 0, 0)),
        ],
        out_specs=pl.BlockSpec((rows, tile_cols), lambda c: (0, c)),
        out_shape=jax.ShapeDtypeStruct((rows, cols), jnp.bfloat16),
    )(prev, mid, nxt, terms_local)


def per_device(image_masses, dual_multipliers, fraction_tops, banded_submatrices, band_starts, nslab):
    width = banded_submatrices.shape[2]
    rows = image_masses.shape[1]
    local_blocks = rows // width
    halo = HALO * width
    slab = lax.axis_index("slab")

    terms = offset_terms(banded_submatrices, band_starts)
    terms_local = lax.dynamic_slice_in_dim(terms, slab * local_blocks, local_blocks, axis=0)

    total_weight = lax.psum(jnp.sum(fraction_tops).astype(jnp.float32), "img")
    weight = fraction_tops.astype(jnp.float32)[0]

    up = [(i, i + 1) for i in range(nslab - 1)]
    down = [(i + 1, i) for i in range(nslab - 1)]

    def exchange(inner):
        to_up = inner[rows - halo :]
        to_down = inner[:halo]
        if nslab != 4:
            return lax.ppermute(to_up, "slab", up), lax.ppermute(to_down, "slab", down)
        half = halo // 2
        direct_prev = lax.ppermute(to_up, "slab", [(0, 1), (2, 3)])
        direct_next = lax.ppermute(to_down, "slab", [(1, 0), (3, 2)])
        first = jnp.where(slab == 1, to_up[:half], to_down[:half])
        second = jnp.where(slab == 1, to_up[half:], to_down[half:])
        first = lax.ppermute(first, "slab", [(1, 3), (2, 0)])
        second = lax.ppermute(second, "slab", [(1, 0), (2, 3)])
        first = lax.ppermute(first, "slab", [(3, 2), (0, 1)])
        second = lax.ppermute(second, "slab", [(0, 2), (3, 1)])
        diagonal = jnp.concatenate([first, second], axis=0)
        return jnp.where(slab == 2, diagonal, direct_prev), jnp.where(slab == 1, diagonal, direct_next)

    def apply_kernel(field):
        inner = column_pass(field, terms)
        from_prev, from_next = exchange(inner)
        return row_pass(from_prev, inner, from_next, terms_local)

    masses = image_masses[0]
    scaling = dual_multipliers[0]
    barycenter = None
    for iteration in range(ITERS):
        kernel_v = apply_kernel(scaling.astype(jnp.bfloat16))
        scaled_u = (masses / kernel_v.astype(jnp.float32)).astype(jnp.bfloat16)
        kernel_u = apply_kernel(scaled_u).astype(jnp.float32)
        value_portion = weight * jnp.log(kernel_u)
        log_sum = lax.psum_scatter(value_portion, "img", scatter_dimension=0, tiled=True)
        barycenter = lax.all_gather(jnp.exp(log_sum / total_weight), "img", axis=0, tiled=True)
        scaling = barycenter / kernel_u
    return (barycenter, scaling[None])


def solution(mesh):
    nslab = mesh.shape["slab"]
    placed = (P("img", "slab", None), P("img", "slab", None), P("img"), P(), P())

    def body(*args):
        return per_device(*args, nslab=nslab)

    return jax.shard_map(
        body,
        mesh=mesh,
        in_specs=placed,
        out_specs=(P("slab", None), P("img", "slab", None)),
        check_vma=False,
    )
```

```python
import functools

import jax
import jax.numpy as jnp
from jax import lax
from jax.experimental import pallas as pl
import numpy as np
from jax.sharding import PartitionSpec as P

ITERS = 2
HALO = 2
OFFSETS = 2 * HALO + 1


def window_starts(nblocks, group):
    span = group + 2 * HALO
    return [min(max(g * group - HALO, 0), nblocks - span) for g in range(nblocks // group)]


def column_terms(banded_submatrices, band_starts, group):
    nblocks, _, width, _ = banded_submatrices.shape
    span = group + 2 * HALO
    ngroups = nblocks // group
    rows = np.arange(nblocks).reshape(ngroups, group)
    cols = np.array(window_starts(nblocks, group))[:, None] + np.arange(span)[None, :]
    target = rows[:, :, None] + band_starts[rows]
    matches = cols[:, None, :, None] == target[:, :, None, :]
    blocks = banded_submatrices[rows]
    terms = jnp.einsum(
        "gbcj,gbjik->gckbi", matches.astype(jnp.bfloat16), blocks, preferred_element_type=jnp.float32
    ).astype(jnp.bfloat16)
    return terms.reshape((ngroups, span * width, group * width))


def row_terms(banded_submatrices, band_starts, first, local_blocks, group):
    nblocks, _, width, _ = banded_submatrices.shape
    span = group + 2 * HALO
    ngroups = local_blocks // group
    local_rows = np.arange(local_blocks).reshape(ngroups, group)
    block_rows = lax.dynamic_slice_in_dim(banded_submatrices, first, local_blocks, axis=0)[local_rows]
    starts = lax.dynamic_slice_in_dim(band_starts, first, local_blocks, axis=0)[local_rows]
    cols = first + (local_rows[:, :1] - HALO + np.arange(span)[None, :])
    in_range = (cols >= 0) & (cols < nblocks)
    target = first + local_rows[:, :, None] + starts
    matches = (cols[:, None, :, None] == target[:, :, None, :]) & in_range[:, None, :, None]
    terms = jnp.einsum(
        "gbej,gbjik->gbiek", matches.astype(jnp.bfloat16), block_rows, preferred_element_type=jnp.float32
    ).astype(jnp.bfloat16)
    return terms.reshape((ngroups, group * width, span * width))


def column_kernel(x_ref, t_ref, o_ref, *, group, width):
    nblocks = x_ref.shape[1] // width
    span = group + 2 * HALO
    x = x_ref[...].astype(jnp.bfloat16)
    for g, first in enumerate(window_starts(nblocks, group)):
        window = x[:, first * width : (first + span) * width]
        out = jnp.dot(window, t_ref[g], preferred_element_type=jnp.float32)
        o_ref[:, g * group * width : (g + 1) * group * width] = out.astype(o_ref.dtype)


def column_pass(field, terms, group, width, tile_rows=256):
    rows, cols = field.shape
    return pl.pallas_call(
        functools.partial(column_kernel, group=group, width=width),
        grid=(rows // tile_rows,),
        in_specs=[
            pl.BlockSpec((tile_rows, cols), lambda r: (r, 0)),
            pl.BlockSpec(terms.shape, lambda r: (0, 0, 0)),
        ],
        out_specs=pl.BlockSpec((tile_rows, cols), lambda r: (r, 0)),
        out_shape=jax.ShapeDtypeStruct((rows, cols), jnp.bfloat16),
    )(field, terms)


def row_kernel(prev_ref, mid_ref, next_ref, t_ref, o_ref, *, group, width):
    local_blocks = mid_ref.shape[0] // width
    span = group + 2 * HALO
    sources = [(prev_ref, 0, HALO), (mid_ref, HALO, HALO + local_blocks), (next_ref, HALO + local_blocks, 2 * HALO + local_blocks)]
    for g in range(local_blocks // group):
        lo = g * group
        acc = None
        for ref, start, stop in sources:
            a, b = max(lo, start), min(lo + span, stop)
            if a >= b:
                continue
            src = ref[(a - start) * width : (b - start) * width, :]
            prod = jnp.dot(t_ref[g, :, (a - lo) * width : (b - lo) * width], src, preferred_element_type=jnp.float32)
            acc = prod if acc is None else acc + prod
        o_ref[lo * width : (lo + group) * width, :] = acc.astype(o_ref.dtype)


def row_pass(prev, mid, nxt, terms_local, group, width, tile_cols=768):
    rows, cols = mid.shape
    halo_rows = prev.shape[0]
    return pl.pallas_call(
        functools.partial(row_kernel, group=group, width=width),
        grid=(cols // tile_cols,),
        in_specs=[
            pl.BlockSpec((halo_rows, tile_cols), lambda c: (0, c)),
            pl.BlockSpec((rows, tile_cols), lambda c: (0, c)),
            pl.BlockSpec((halo_rows, tile_cols), lambda c: (0, c)),
            pl.BlockSpec(terms_local.shape, lambda c: (0, 0, 0)),
        ],
        out_specs=pl.BlockSpec((rows, tile_cols), lambda c: (0, c)),
        out_shape=jax.ShapeDtypeStruct((rows, cols), jnp.bfloat16),
    )(prev, mid, nxt, terms_local)


def per_device(image_masses, dual_multipliers, fraction_tops, banded_submatrices, band_starts, nslab):
    width = banded_submatrices.shape[2]
    rows = image_masses.shape[1]
    local_blocks = rows // width
    halo = HALO * width
    slab = lax.axis_index("slab")

    nblocks = banded_submatrices.shape[0]
    col_group = 2 if nblocks % 2 == 0 and nblocks >= 2 + 2 * HALO else 1
    row_group = 2 if local_blocks % 2 == 0 else 1
    terms = column_terms(banded_submatrices, band_starts, col_group)
    terms_local = row_terms(banded_submatrices, band_starts, slab * local_blocks, local_blocks, row_group)

    total_weight = lax.psum(jnp.sum(fraction_tops).astype(jnp.float32), "img")
    weight = fraction_tops.astype(jnp.float32)[0]

    up = [(i, i + 1) for i in range(nslab - 1)]
    down = [(i + 1, i) for i in range(nslab - 1)]

    def exchange(inner):
        to_up = inner[rows - halo :]
        to_down = inner[:halo]
        if nslab != 4:
            return lax.ppermute(to_up, "slab", up), lax.ppermute(to_down, "slab", down)
        half = halo // 2
        direct_prev = lax.ppermute(to_up, "slab", [(0, 1), (2, 3)])
        direct_next = lax.ppermute(to_down, "slab", [(1, 0), (3, 2)])
        first = jnp.where(slab == 1, to_up[:half], to_down[:half])
        second = jnp.where(slab == 1, to_up[half:], to_down[half:])
        first = lax.ppermute(first, "slab", [(1, 3), (2, 0)])
        second = lax.ppermute(second, "slab", [(1, 0), (2, 3)])
        first = lax.ppermute(first, "slab", [(3, 2), (0, 1)])
        second = lax.ppermute(second, "slab", [(0, 2), (3, 1)])
        diagonal = jnp.concatenate([first, second], axis=0)
        return jnp.where(slab == 2, diagonal, direct_prev), jnp.where(slab == 1, diagonal, direct_next)

    def apply_kernel(field):
        inner = column_pass(field, terms, col_group, width)
        from_prev, from_next = exchange(inner)
        return row_pass(from_prev, inner, from_next, terms_local, row_group, width)

    masses = image_masses[0]
    scaling = dual_multipliers[0]
    barycenter = None
    for iteration in range(ITERS):
        kernel_v = apply_kernel(scaling.astype(jnp.bfloat16))
        scaled_u = (masses / kernel_v.astype(jnp.float32)).astype(jnp.bfloat16)
        kernel_u = apply_kernel(scaled_u).astype(jnp.float32)
        value_portion = weight * jnp.log(kernel_u)
        log_sum = lax.psum_scatter(value_portion, "img", scatter_dimension=0, tiled=True)
        barycenter = lax.all_gather(jnp.exp(log_sum / total_weight), "img", axis=0, tiled=True)
        scaling = barycenter / kernel_u
    return (barycenter, scaling[None])


def solution(mesh):
    nslab = mesh.shape["slab"]
    placed = (P("img", "slab", None), P("img", "slab", None), P("img"), P(), P())

    def body(*args):
        return per_device(*args, nslab=nslab)

    return jax.shard_map(
        body,
        mesh=mesh,
        in_specs=placed,
        out_specs=(P("slab", None), P("img", "slab", None)),
        check_vma=False,
    )
```

```python
import functools

import jax
import jax.numpy as jnp
from jax import lax
from jax.experimental import pallas as pl
import numpy as np
from jax.sharding import PartitionSpec as P

ITERS = 2
HALO = 2
OFFSETS = 2 * HALO + 1


def window_starts(nblocks, group):
    span = group + 2 * HALO
    return [min(max(g * group - HALO, 0), nblocks - span) for g in range(nblocks // group)]


def column_terms(banded_submatrices, band_starts, group):
    nblocks, _, width, _ = banded_submatrices.shape
    span = group + 2 * HALO
    ngroups = nblocks // group
    rows = np.arange(nblocks).reshape(ngroups, group)
    cols = np.array(window_starts(nblocks, group))[:, None] + np.arange(span)[None, :]
    target = rows[:, :, None] + band_starts[rows]
    matches = cols[:, None, :, None] == target[:, :, None, :]
    blocks = banded_submatrices[rows]
    terms = jnp.einsum(
        "gbcj,gbjik->gckbi", matches.astype(jnp.bfloat16), blocks, preferred_element_type=jnp.float32
    ).astype(jnp.bfloat16)
    return terms.reshape((ngroups, span * width, group * width))


def row_terms(banded_submatrices, band_starts, first, local_blocks, group):
    nblocks, _, width, _ = banded_submatrices.shape
    span = group + 2 * HALO
    ngroups = local_blocks // group
    local_rows = np.arange(local_blocks).reshape(ngroups, group)
    block_rows = lax.dynamic_slice_in_dim(banded_submatrices, first, local_blocks, axis=0)[local_rows]
    starts = lax.dynamic_slice_in_dim(band_starts, first, local_blocks, axis=0)[local_rows]
    cols = first + (local_rows[:, :1] - HALO + np.arange(span)[None, :])
    in_range = (cols >= 0) & (cols < nblocks)
    target = first + local_rows[:, :, None] + starts
    matches = (cols[:, None, :, None] == target[:, :, None, :]) & in_range[:, None, :, None]
    terms = jnp.einsum(
        "gbej,gbjik->gbiek", matches.astype(jnp.bfloat16), block_rows, preferred_element_type=jnp.float32
    ).astype(jnp.bfloat16)
    return terms.reshape((ngroups, group * width, span * width))


def column_kernel(x_ref, t_ref, o_ref, *, group, width):
    nblocks = x_ref.shape[1] // width
    span = group + 2 * HALO
    x = x_ref[...].astype(jnp.bfloat16)
    for g, first in enumerate(window_starts(nblocks, group)):
        window = x[:, first * width : (first + span) * width]
        out = jnp.dot(window, t_ref[g], preferred_element_type=jnp.float32)
        o_ref[:, g * group * width : (g + 1) * group * width] = out.astype(o_ref.dtype)


def column_pass(field, terms, group, width, tile_rows=128):
    rows, cols = field.shape
    return pl.pallas_call(
        functools.partial(column_kernel, group=group, width=width),
        grid=(rows // tile_rows,),
        in_specs=[
            pl.BlockSpec((tile_rows, cols), lambda r: (r, 0)),
            pl.BlockSpec(terms.shape, lambda r: (0, 0, 0)),
        ],
        out_specs=pl.BlockSpec((tile_rows, cols), lambda r: (r, 0)),
        out_shape=jax.ShapeDtypeStruct((rows, cols), jnp.bfloat16),
    )(field, terms)


def row_kernel(prev_ref, mid_ref, next_ref, t_ref, o_ref, *, group, width):
    local_blocks = mid_ref.shape[0] // width
    span = group + 2 * HALO
    sources = [(prev_ref, 0, HALO), (mid_ref, HALO, HALO + local_blocks), (next_ref, HALO + local_blocks, 2 * HALO + local_blocks)]
    for g in range(local_blocks // group):
        lo = g * group
        acc = None
        for ref, start, stop in sources:
            a, b = max(lo, start), min(lo + span, stop)
            if a >= b:
                continue
            src = ref[(a - start) * width : (b - start) * width, :]
            prod = jnp.dot(t_ref[g, :, (a - lo) * width : (b - lo) * width], src, preferred_element_type=jnp.float32)
            acc = prod if acc is None else acc + prod
        o_ref[lo * width : (lo + group) * width, :] = acc.astype(o_ref.dtype)


def row_pass(prev, mid, nxt, terms_local, group, width, tile_cols=384):
    rows, cols = mid.shape
    halo_rows = prev.shape[0]
    return pl.pallas_call(
        functools.partial(row_kernel, group=group, width=width),
        grid=(cols // tile_cols,),
        in_specs=[
            pl.BlockSpec((halo_rows, tile_cols), lambda c: (0, c)),
            pl.BlockSpec((rows, tile_cols), lambda c: (0, c)),
            pl.BlockSpec((halo_rows, tile_cols), lambda c: (0, c)),
            pl.BlockSpec(terms_local.shape, lambda c: (0, 0, 0)),
        ],
        out_specs=pl.BlockSpec((rows, tile_cols), lambda c: (0, c)),
        out_shape=jax.ShapeDtypeStruct((rows, cols), jnp.bfloat16),
    )(prev, mid, nxt, terms_local)


def per_device(image_masses, dual_multipliers, fraction_tops, banded_submatrices, band_starts, nslab):
    width = banded_submatrices.shape[2]
    rows = image_masses.shape[1]
    local_blocks = rows // width
    halo = HALO * width
    slab = lax.axis_index("slab")

    nblocks = banded_submatrices.shape[0]
    col_group = 2 if nblocks % 2 == 0 and nblocks >= 2 + 2 * HALO else 1
    row_group = 2 if local_blocks % 2 == 0 else 1
    terms = column_terms(banded_submatrices, band_starts, col_group)
    terms_local = row_terms(banded_submatrices, band_starts, slab * local_blocks, local_blocks, row_group)

    total_weight = lax.psum(jnp.sum(fraction_tops).astype(jnp.float32), "img")
    weight = fraction_tops.astype(jnp.float32)[0]

    up = [(i, i + 1) for i in range(nslab - 1)]
    down = [(i + 1, i) for i in range(nslab - 1)]

    def exchange(inner):
        to_up = inner[rows - halo :]
        to_down = inner[:halo]
        if nslab != 4:
            return lax.ppermute(to_up, "slab", up), lax.ppermute(to_down, "slab", down)
        half = halo // 2
        direct_prev = lax.ppermute(to_up, "slab", [(0, 1), (2, 3)])
        direct_next = lax.ppermute(to_down, "slab", [(1, 0), (3, 2)])
        first = jnp.where(slab == 1, to_up[:half], to_down[:half])
        second = jnp.where(slab == 1, to_up[half:], to_down[half:])
        first = lax.ppermute(first, "slab", [(1, 3), (2, 0)])
        second = lax.ppermute(second, "slab", [(1, 0), (2, 3)])
        first = lax.ppermute(first, "slab", [(3, 2), (0, 1)])
        second = lax.ppermute(second, "slab", [(0, 2), (3, 1)])
        diagonal = jnp.concatenate([first, second], axis=0)
        return jnp.where(slab == 2, diagonal, direct_prev), jnp.where(slab == 1, diagonal, direct_next)

    def apply_kernel(field):
        inner = column_pass(field, terms, col_group, width)
        from_prev, from_next = exchange(inner)
        return row_pass(from_prev, inner, from_next, terms_local, row_group, width)

    masses = image_masses[0]
    scaling = dual_multipliers[0]
    barycenter = None
    for iteration in range(ITERS):
        kernel_v = apply_kernel(scaling.astype(jnp.bfloat16))
        scaled_u = (masses / kernel_v.astype(jnp.float32)).astype(jnp.bfloat16)
        kernel_u = apply_kernel(scaled_u).astype(jnp.float32)
        value_portion = weight * jnp.log(kernel_u)
        log_sum = lax.psum_scatter(value_portion, "img", scatter_dimension=0, tiled=True)
        barycenter = lax.all_gather(jnp.exp(log_sum / total_weight), "img", axis=0, tiled=True)
        scaling = barycenter / kernel_u
    return (barycenter, scaling[None])


def solution(mesh):
    nslab = mesh.shape["slab"]
    placed = (P("img", "slab", None), P("img", "slab", None), P("img"), P(), P())

    def body(*args):
        return per_device(*args, nslab=nslab)

    return jax.shard_map(
        body,
        mesh=mesh,
        in_specs=placed,
        out_specs=(P("slab", None), P("img", "slab", None)),
        check_vma=False,
    )
```

```python
import functools

import jax
import jax.numpy as jnp
from jax import lax
from jax.experimental import pallas as pl
from jax.sharding import PartitionSpec as P

ITERS = 2
HALO = 2
OFFSETS = 2 * HALO + 1


def offset_terms(banded_submatrices, band_starts):
    offsets = jnp.arange(-HALO, HALO + 1, dtype=jnp.int32)
    matches = band_starts[:, None, :] == offsets[None, :, None]
    picked = jnp.where(matches[:, :, :, None, None], banded_submatrices[:, None], jnp.zeros((), jnp.bfloat16))
    return jnp.sum(picked, axis=2)


def column_kernel(x_ref, t_ref, o_ref):
    nblocks = t_ref.shape[0]
    width = t_ref.shape[2]
    x = x_ref[...].astype(jnp.bfloat16)
    for b in range(nblocks):
        acc = None
        for o in range(OFFSETS):
            c = b + o - HALO
            if c < 0 or c >= nblocks:
                continue
            prod = lax.dot_general(
                x[:, c * width : (c + 1) * width],
                t_ref[b, o],
                (((1,), (1,)), ((), ())),
                preferred_element_type=jnp.float32,
            )
            acc = prod if acc is None else acc + prod
        o_ref[:, b * width : (b + 1) * width] = acc.astype(o_ref.dtype)


def column_pass(field, terms, tile_rows=256):
    rows, cols = field.shape
    return pl.pallas_call(
        column_kernel,
        grid=(rows // tile_rows,),
        in_specs=[
            pl.BlockSpec((tile_rows, cols), lambda r: (r, 0)),
            pl.BlockSpec(terms.shape, lambda r: (0, 0, 0, 0)),
        ],
        out_specs=pl.BlockSpec((tile_rows, cols), lambda r: (r, 0)),
        out_shape=jax.ShapeDtypeStruct((rows, cols), jnp.bfloat16),
    )(field, terms)


def row_kernel(*refs, blocks, has_halo):
    if has_halo:
        prev_ref, mid_ref, next_ref, t_ref, o_ref = refs
    else:
        mid_ref, t_ref, o_ref = refs
    nlocal = t_ref.shape[0]
    width = t_ref.shape[2]
    for i, b in enumerate(blocks):
        acc = None
        for o in range(OFFSETS):
            e = b + o - HALO
            if e < 0:
                src = prev_ref[(e + HALO) * width : (e + HALO + 1) * width, :]
            elif e >= nlocal:
                src = next_ref[(e - nlocal) * width : (e - nlocal + 1) * width, :]
            else:
                src = mid_ref[e * width : (e + 1) * width, :]
            prod = jnp.dot(t_ref[b, o], src, preferred_element_type=jnp.float32)
            acc = prod if acc is None else acc + prod
        o_ref[i * width : (i + 1) * width, :] = acc.astype(o_ref.dtype)


def row_pass(mid, terms_local, blocks, halos=None, tile_cols=768):
    rows, cols = mid.shape
    width = terms_local.shape[2]
    tile = lambda r: pl.BlockSpec((r, tile_cols), lambda c: (0, c))
    operands = [mid, terms_local]
    specs = [tile(rows), pl.BlockSpec(terms_local.shape, lambda c: (0, 0, 0, 0))]
    if halos is not None:
        prev, nxt = halos
        operands = [prev, mid, nxt, terms_local]
        specs = [tile(prev.shape[0]), tile(rows), tile(nxt.shape[0]), specs[1]]
    return pl.pallas_call(
        functools.partial(row_kernel, blocks=tuple(blocks), has_halo=halos is not None),
        grid=(cols // tile_cols,),
        in_specs=specs,
        out_specs=tile(len(blocks) * width),
        out_shape=jax.ShapeDtypeStruct((len(blocks) * width, cols), jnp.bfloat16),
    )(*operands)


def per_device(image_masses, dual_multipliers, fraction_tops, banded_submatrices, band_starts, nslab):
    width = banded_submatrices.shape[2]
    rows = image_masses.shape[1]
    local_blocks = rows // width
    halo = HALO * width
    slab = lax.axis_index("slab")

    terms = offset_terms(banded_submatrices, band_starts)
    terms_local = lax.dynamic_slice_in_dim(terms, slab * local_blocks, local_blocks, axis=0)

    total_weight = lax.psum(jnp.sum(fraction_tops).astype(jnp.float32), "img")
    weight = fraction_tops.astype(jnp.float32)[0]

    up = [(i, i + 1) for i in range(nslab - 1)]
    down = [(i + 1, i) for i in range(nslab - 1)]

    def exchange(inner):
        to_up = inner[rows - halo :]
        to_down = inner[:halo]
        if nslab != 4:
            return lax.ppermute(to_up, "slab", up), lax.ppermute(to_down, "slab", down)
        half = halo // 2
        direct_prev = lax.ppermute(to_up, "slab", [(0, 1), (2, 3)])
        direct_next = lax.ppermute(to_down, "slab", [(1, 0), (3, 2)])
        first = jnp.where(slab == 1, to_up[:half], to_down[:half])
        second = jnp.where(slab == 1, to_up[half:], to_down[half:])
        first = lax.ppermute(first, "slab", [(1, 3), (2, 0)])
        second = lax.ppermute(second, "slab", [(1, 0), (2, 3)])
        first = lax.ppermute(first, "slab", [(3, 2), (0, 1)])
        second = lax.ppermute(second, "slab", [(0, 2), (3, 1)])
        diagonal = jnp.concatenate([first, second], axis=0)
        return jnp.where(slab == 2, diagonal, direct_prev), jnp.where(slab == 1, diagonal, direct_next)

    all_blocks = list(range(local_blocks))
    interior = all_blocks[HALO : local_blocks - HALO]
    boundary = all_blocks[:HALO] + all_blocks[local_blocks - HALO :] if interior else all_blocks

    def apply_kernel(field):
        inner = column_pass(field, terms)
        return row_pass(inner, terms_local, all_blocks, exchange(inner))

    def log_barycenter(kernel_u):
        value_portion = weight * jnp.log(kernel_u)
        log_sum = lax.psum_scatter(value_portion, "img", scatter_dimension=0, tiled=True)
        return lax.all_gather(jnp.exp(log_sum / total_weight), "img", axis=0, tiled=True)

    def final_apply(field):
        inner = column_pass(field, terms)
        halos = exchange(inner)
        if not interior:
            kernel_u = row_pass(inner, terms_local, all_blocks, halos).astype(jnp.float32)
            return kernel_u, log_barycenter(kernel_u)
        inside = row_pass(inner, terms_local, interior).astype(jnp.float32)
        inside_sum = lax.psum_scatter(weight * jnp.log(inside), "img", scatter_dimension=0, tiled=True)
        halos, inside_sum = lax.optimization_barrier((halos, inside_sum))
        inside_bary = lax.all_gather(jnp.exp(inside_sum / total_weight), "img", axis=0, tiled=True)
        edges = row_pass(inner, terms_local, boundary, halos).astype(jnp.float32)
        edges_bary = log_barycenter(edges)
        cut = HALO * width
        kernel_u = jnp.concatenate([edges[:cut], inside, edges[cut:]], axis=0)
        barycenter = jnp.concatenate([edges_bary[:cut], inside_bary, edges_bary[cut:]], axis=0)
        return kernel_u, barycenter

    masses = image_masses[0]
    scaling = dual_multipliers[0]
    barycenter = None
    for iteration in range(ITERS):
        kernel_v = apply_kernel(scaling.astype(jnp.bfloat16))
        scaled_u = (masses / kernel_v.astype(jnp.float32)).astype(jnp.bfloat16)
        kernel_u, barycenter = final_apply(scaled_u)
        scaling = barycenter / kernel_u
    return (barycenter, scaling[None])


def solution(mesh):
    nslab = mesh.shape["slab"]
    placed = (P("img", "slab", None), P("img", "slab", None), P("img"), P(), P())

    def body(*args):
        return per_device(*args, nslab=nslab)

    return jax.shard_map(
        body,
        mesh=mesh,
        in_specs=placed,
        out_specs=(P("slab", None), P("img", "slab", None)),
        check_vma=False,
    )
```

```python
import functools

import jax
import jax.numpy as jnp
from jax import lax
from jax.experimental import pallas as pl
from jax.sharding import PartitionSpec as P

ITERS = 2
HALO = 2
OFFSETS = 2 * HALO + 1


def offset_terms(banded_submatrices, band_starts):
    offsets = jnp.arange(-HALO, HALO + 1, dtype=jnp.int32)
    matches = band_starts[:, None, :] == offsets[None, :, None]
    picked = jnp.where(matches[:, :, :, None, None], banded_submatrices[:, None], jnp.zeros((), jnp.bfloat16))
    return jnp.sum(picked, axis=2)


def column_kernel(x_ref, t_ref, o_ref):
    nblocks = t_ref.shape[0]
    width = t_ref.shape[2]
    x = x_ref[...].astype(jnp.bfloat16)
    for b in range(nblocks):
        acc = None
        for o in range(OFFSETS):
            c = b + o - HALO
            if c < 0 or c >= nblocks:
                continue
            prod = lax.dot_general(
                x[:, c * width : (c + 1) * width],
                t_ref[b, o],
                (((1,), (1,)), ((), ())),
                preferred_element_type=jnp.float32,
            )
            acc = prod if acc is None else acc + prod
        o_ref[:, b * width : (b + 1) * width] = acc.astype(o_ref.dtype)


def column_pass(field, terms, tile_rows=256):
    rows, cols = field.shape
    return pl.pallas_call(
        column_kernel,
        grid=(rows // tile_rows,),
        in_specs=[
            pl.BlockSpec((tile_rows, cols), lambda r: (r, 0)),
            pl.BlockSpec(terms.shape, lambda r: (0, 0, 0, 0)),
        ],
        out_specs=pl.BlockSpec((tile_rows, cols), lambda r: (r, 0)),
        out_shape=jax.ShapeDtypeStruct((rows, cols), jnp.bfloat16),
    )(field, terms)


def row_kernel(*refs, blocks, has_halo):
    if has_halo:
        prev_ref, mid_ref, next_ref, t_ref, o_ref = refs
    else:
        mid_ref, t_ref, o_ref = refs
    nlocal = t_ref.shape[0]
    width = t_ref.shape[2]
    for i, b in enumerate(blocks):
        acc = None
        for o in range(OFFSETS):
            e = b + o - HALO
            if e < 0:
                src = prev_ref[(e + HALO) * width : (e + HALO + 1) * width, :]
            elif e >= nlocal:
                src = next_ref[(e - nlocal) * width : (e - nlocal + 1) * width, :]
            else:
                src = mid_ref[e * width : (e + 1) * width, :]
            prod = jnp.dot(t_ref[b, o], src, preferred_element_type=jnp.float32)
            acc = prod if acc is None else acc + prod
        o_ref[i * width : (i + 1) * width, :] = acc.astype(o_ref.dtype)


def row_pass(mid, terms_local, blocks, halos=None, tile_cols=768):
    rows, cols = mid.shape
    width = terms_local.shape[2]
    tile = lambda r: pl.BlockSpec((r, tile_cols), lambda c: (0, c))
    operands = [mid, terms_local]
    specs = [tile(rows), pl.BlockSpec(terms_local.shape, lambda c: (0, 0, 0, 0))]
    if halos is not None:
        prev, nxt = halos
        operands = [prev, mid, nxt, terms_local]
        specs = [tile(prev.shape[0]), tile(rows), tile(nxt.shape[0]), specs[1]]
    return pl.pallas_call(
        functools.partial(row_kernel, blocks=tuple(blocks), has_halo=halos is not None),
        grid=(cols // tile_cols,),
        in_specs=specs,
        out_specs=tile(len(blocks) * width),
        out_shape=jax.ShapeDtypeStruct((len(blocks) * width, cols), jnp.bfloat16),
    )(*operands)


def per_device(image_masses, dual_multipliers, fraction_tops, banded_submatrices, band_starts, nslab):
    width = banded_submatrices.shape[2]
    rows = image_masses.shape[1]
    local_blocks = rows // width
    halo = HALO * width
    slab = lax.axis_index("slab")

    terms = offset_terms(banded_submatrices, band_starts)
    terms_local = lax.dynamic_slice_in_dim(terms, slab * local_blocks, local_blocks, axis=0)

    total_weight = lax.psum(jnp.sum(fraction_tops).astype(jnp.float32), "img")
    weight = fraction_tops.astype(jnp.float32)[0]

    up = [(i, i + 1) for i in range(nslab - 1)]
    down = [(i + 1, i) for i in range(nslab - 1)]

    def exchange(to_up, to_down):
        if nslab != 4:
            return lax.ppermute(to_up, "slab", up), lax.ppermute(to_down, "slab", down)
        half = halo // 2
        direct_prev = lax.ppermute(to_up, "slab", [(0, 1), (2, 3)])
        direct_next = lax.ppermute(to_down, "slab", [(1, 0), (3, 2)])
        first = jnp.where(slab == 1, to_up[:half], to_down[:half])
        second = jnp.where(slab == 1, to_up[half:], to_down[half:])
        first = lax.ppermute(first, "slab", [(1, 3), (2, 0)])
        second = lax.ppermute(second, "slab", [(1, 0), (2, 3)])
        first = lax.ppermute(first, "slab", [(3, 2), (0, 1)])
        second = lax.ppermute(second, "slab", [(0, 2), (3, 1)])
        diagonal = jnp.concatenate([first, second], axis=0)
        return jnp.where(slab == 2, diagonal, direct_prev), jnp.where(slab == 1, diagonal, direct_next)

    all_blocks = list(range(local_blocks))
    interior = all_blocks[HALO : local_blocks - HALO]
    boundary = all_blocks[:HALO] + all_blocks[local_blocks - HALO :] if interior else all_blocks

    def apply_kernel(field):
        inner = column_pass(field, terms)
        return row_pass(inner, terms_local, all_blocks, exchange(inner[rows - halo :], inner[:halo]))

    def apply_split(edges, inside):
        inner_edges = column_pass(edges, terms)
        halos = exchange(inner_edges[halo:], inner_edges[:halo])
        inner = jnp.concatenate([inner_edges[:halo], column_pass(inside, terms), inner_edges[halo:]], axis=0)
        return row_pass(inner, terms_local, all_blocks, halos)

    def log_sum(kernel_u):
        return lax.psum_scatter(weight * jnp.log(kernel_u), "img", scatter_dimension=0, tiled=True)

    def gather_barycenter(part_sum):
        return lax.all_gather(jnp.exp(part_sum / total_weight), "img", axis=0, tiled=True)

    def final_apply(field):
        inner = column_pass(field, terms)
        halos = exchange(inner[rows - halo :], inner[:halo])
        if not interior:
            kernel_u = row_pass(inner, terms_local, all_blocks, halos).astype(jnp.float32)
            return kernel_u, gather_barycenter(log_sum(kernel_u))
        inside = row_pass(inner, terms_local, interior).astype(jnp.float32)
        inside_sum = log_sum(inside)
        halos, inside_sum = lax.optimization_barrier((halos, inside_sum))
        edges = row_pass(inner, terms_local, boundary, halos).astype(jnp.float32)
        edges_bary = gather_barycenter(log_sum(edges))
        edges_bary, inside_sum = lax.optimization_barrier((edges_bary, inside_sum))
        inside_bary = gather_barycenter(inside_sum)
        return (edges, inside), (edges_bary, inside_bary)

    def assemble(parts):
        edges, inside = parts
        return jnp.concatenate([edges[:halo], inside, edges[halo:]], axis=0)

    masses = image_masses[0]
    scaling = dual_multipliers[0]
    kernel_v = apply_kernel(scaling.astype(jnp.bfloat16))
    for iteration in range(ITERS):
        if iteration:
            if interior:
                side_edges, side_inside = [(b / k).astype(jnp.bfloat16) for b, k in zip(barycenter, kernel_u)]
                kernel_v = apply_split(side_edges, side_inside)
            else:
                kernel_v = apply_kernel((barycenter / kernel_u).astype(jnp.bfloat16))
        scaled_u = (masses / kernel_v.astype(jnp.float32)).astype(jnp.bfloat16)
        kernel_u, barycenter = final_apply(scaled_u)
    if interior:
        kernel_u, barycenter = assemble(kernel_u), assemble(barycenter)
    return (barycenter, (barycenter / kernel_u)[None])


def solution(mesh):
    nslab = mesh.shape["slab"]
    placed = (P("img", "slab", None), P("img", "slab", None), P("img"), P(), P())

    def body(*args):
        return per_device(*args, nslab=nslab)

    return jax.shard_map(
        body,
        mesh=mesh,
        in_specs=placed,
        out_specs=(P("slab", None), P("img", "slab", None)),
        check_vma=False,
    )
```

```python
import functools

import jax
import jax.numpy as jnp
from jax import lax
from jax.experimental import pallas as pl
from jax.sharding import PartitionSpec as P

ITERS = 2
HALO = 2
OFFSETS = 2 * HALO + 1


def offset_terms(banded_submatrices, band_starts):
    offsets = jnp.arange(-HALO, HALO + 1, dtype=jnp.int32)
    matches = band_starts[:, None, :] == offsets[None, :, None]
    picked = jnp.where(matches[:, :, :, None, None], banded_submatrices[:, None], jnp.zeros((), jnp.bfloat16))
    return jnp.sum(picked, axis=2)


def column_kernel(*refs):
    *in_refs, t_ref, o_ref = refs
    nblocks = t_ref.shape[0]
    width = t_ref.shape[2]
    if len(in_refs) == 2:
        x = (in_refs[0][...] / in_refs[1][...].astype(jnp.float32)).astype(jnp.bfloat16)
    else:
        x = in_refs[0][...].astype(jnp.bfloat16)
    for b in range(nblocks):
        acc = None
        for o in range(OFFSETS):
            c = b + o - HALO
            if c < 0 or c >= nblocks:
                continue
            prod = lax.dot_general(
                x[:, c * width : (c + 1) * width],
                t_ref[b, o],
                (((1,), (1,)), ((), ())),
                preferred_element_type=jnp.float32,
            )
            acc = prod if acc is None else acc + prod
        o_ref[:, b * width : (b + 1) * width] = acc.astype(o_ref.dtype)


def column_pass(fields, terms, tile_rows=256):
    fields = fields if isinstance(fields, tuple) else (fields,)
    rows, cols = fields[0].shape
    tile = pl.BlockSpec((tile_rows, cols), lambda r: (r, 0))
    return pl.pallas_call(
        column_kernel,
        grid=(rows // tile_rows,),
        in_specs=[tile] * len(fields) + [pl.BlockSpec(terms.shape, lambda r: (0, 0, 0, 0))],
        out_specs=tile,
        out_shape=jax.ShapeDtypeStruct((rows, cols), jnp.bfloat16),
    )(*fields, terms)


def row_kernel(*refs, blocks, has_halo):
    if has_halo:
        prev_ref, mid_ref, next_ref, t_ref, o_ref = refs
    else:
        mid_ref, t_ref, o_ref = refs
    nlocal = t_ref.shape[0]
    width = t_ref.shape[2]
    for i, b in enumerate(blocks):
        acc = None
        for o in range(OFFSETS):
            e = b + o - HALO
            if e < 0:
                src = prev_ref[(e + HALO) * width : (e + HALO + 1) * width, :]
            elif e >= nlocal:
                src = next_ref[(e - nlocal) * width : (e - nlocal + 1) * width, :]
            else:
                src = mid_ref[e * width : (e + 1) * width, :]
            prod = jnp.dot(t_ref[b, o], src, preferred_element_type=jnp.float32)
            acc = prod if acc is None else acc + prod
        o_ref[i * width : (i + 1) * width, :] = acc.astype(o_ref.dtype)


def row_pass(mid, terms_local, blocks, halos=None, tile_cols=768):
    rows, cols = mid.shape
    width = terms_local.shape[2]
    tile = lambda r: pl.BlockSpec((r, tile_cols), lambda c: (0, c))
    operands = [mid, terms_local]
    specs = [tile(rows), pl.BlockSpec(terms_local.shape, lambda c: (0, 0, 0, 0))]
    if halos is not None:
        prev, nxt = halos
        operands = [prev, mid, nxt, terms_local]
        specs = [tile(prev.shape[0]), tile(rows), tile(nxt.shape[0]), specs[1]]
    return pl.pallas_call(
        functools.partial(row_kernel, blocks=tuple(blocks), has_halo=halos is not None),
        grid=(cols // tile_cols,),
        in_specs=specs,
        out_specs=tile(len(blocks) * width),
        out_shape=jax.ShapeDtypeStruct((len(blocks) * width, cols), jnp.bfloat16),
    )(*operands)


def per_device(image_masses, dual_multipliers, fraction_tops, banded_submatrices, band_starts, nslab):
    width = banded_submatrices.shape[2]
    rows = image_masses.shape[1]
    local_blocks = rows // width
    halo = HALO * width
    slab = lax.axis_index("slab")

    terms = offset_terms(banded_submatrices, band_starts)
    terms_local = lax.dynamic_slice_in_dim(terms, slab * local_blocks, local_blocks, axis=0)

    total_weight = lax.psum(jnp.sum(fraction_tops).astype(jnp.float32), "img")
    weight = fraction_tops.astype(jnp.float32)[0]

    up = [(i, i + 1) for i in range(nslab - 1)]
    down = [(i + 1, i) for i in range(nslab - 1)]

    def exchange(to_up, to_down):
        if nslab != 4:
            return lax.ppermute(to_up, "slab", up), lax.ppermute(to_down, "slab", down)
        half = halo // 2
        direct_prev = lax.ppermute(to_up, "slab", [(0, 1), (2, 3)])
        direct_next = lax.ppermute(to_down, "slab", [(1, 0), (3, 2)])
        first = jnp.where(slab == 1, to_up[:half], to_down[:half])
        second = jnp.where(slab == 1, to_up[half:], to_down[half:])
        first = lax.ppermute(first, "slab", [(1, 3), (2, 0)])
        second = lax.ppermute(second, "slab", [(1, 0), (2, 3)])
        first = lax.ppermute(first, "slab", [(3, 2), (0, 1)])
        second = lax.ppermute(second, "slab", [(0, 2), (3, 1)])
        diagonal = jnp.concatenate([first, second], axis=0)
        return jnp.where(slab == 2, diagonal, direct_prev), jnp.where(slab == 1, diagonal, direct_next)

    all_blocks = list(range(local_blocks))
    interior = all_blocks[HALO : local_blocks - HALO]
    boundary = all_blocks[:HALO] + all_blocks[local_blocks - HALO :] if interior else all_blocks

    def apply_kernel(field):
        inner = column_pass(field, terms)
        return row_pass(inner, terms_local, all_blocks, exchange(inner[rows - halo :], inner[:halo]))

    def apply_split(edges, inside):
        inner_edges = column_pass(edges, terms)
        halos = exchange(inner_edges[halo:], inner_edges[:halo])
        inner = jnp.concatenate([inner_edges[:halo], column_pass(inside, terms), inner_edges[halo:]], axis=0)
        return row_pass(inner, terms_local, all_blocks, halos)

    def log_sum(kernel_u):
        return lax.psum_scatter(weight * jnp.log(kernel_u), "img", scatter_dimension=0, tiled=True)

    def gather_barycenter(part_sum):
        return lax.all_gather(jnp.exp(part_sum / total_weight), "img", axis=0, tiled=True)

    def final_apply(field):
        inner = column_pass(field, terms)
        halos = exchange(inner[rows - halo :], inner[:halo])
        if not interior:
            kernel_u = row_pass(inner, terms_local, all_blocks, halos).astype(jnp.float32)
            return kernel_u, gather_barycenter(log_sum(kernel_u))
        inside = row_pass(inner, terms_local, interior).astype(jnp.float32)
        inside_sum = log_sum(inside)
        halos, inside_sum = lax.optimization_barrier((halos, inside_sum))
        edges = row_pass(inner, terms_local, boundary, halos).astype(jnp.float32)
        edges_bary = gather_barycenter(log_sum(edges))
        edges_bary, inside_sum = lax.optimization_barrier((edges_bary, inside_sum))
        inside_bary = gather_barycenter(inside_sum)
        return (edges, inside), (edges_bary, inside_bary)

    def assemble(parts):
        edges, inside = parts
        return jnp.concatenate([edges[:halo], inside, edges[halo:]], axis=0)

    masses = image_masses[0]
    scaling = dual_multipliers[0]
    kernel_v = apply_kernel(scaling)
    for iteration in range(ITERS):
        if iteration:
            if interior:
                side_edges, side_inside = [(b / k).astype(jnp.bfloat16) for b, k in zip(barycenter, kernel_u)]
                kernel_v = apply_split(side_edges, side_inside)
            else:
                kernel_v = apply_kernel((barycenter / kernel_u).astype(jnp.bfloat16))
        kernel_u, barycenter = final_apply((masses, kernel_v))
    if interior:
        kernel_u, barycenter = assemble(kernel_u), assemble(barycenter)
    return (barycenter, (barycenter / kernel_u)[None])


def solution(mesh):
    nslab = mesh.shape["slab"]
    placed = (P("img", "slab", None), P("img", "slab", None), P("img"), P(), P())

    def body(*args):
        return per_device(*args, nslab=nslab)

    return jax.shard_map(
        body,
        mesh=mesh,
        in_specs=placed,
        out_specs=(P("slab", None), P("img", "slab", None)),
        check_vma=False,
    )
```

```python
import functools

import jax
import jax.numpy as jnp
from jax import lax
from jax.experimental import pallas as pl
from jax.sharding import PartitionSpec as P

ITERS = 2
HALO = 2
OFFSETS = 2 * HALO + 1


def offset_terms(banded_submatrices, band_starts):
    offsets = jnp.arange(-HALO, HALO + 1, dtype=jnp.int32)
    matches = band_starts[:, None, :] == offsets[None, :, None]
    picked = jnp.where(matches[:, :, :, None, None], banded_submatrices[:, None], jnp.zeros((), jnp.bfloat16))
    return jnp.sum(picked, axis=2)


def column_kernel(*refs):
    *in_refs, t_ref, o_ref = refs
    nblocks = t_ref.shape[0]
    width = t_ref.shape[2]
    if len(in_refs) == 2:
        x = (in_refs[0][...] / in_refs[1][...].astype(jnp.float32)).astype(jnp.bfloat16)
    else:
        x = in_refs[0][...].astype(jnp.bfloat16)
    for b in range(nblocks):
        acc = None
        for o in range(OFFSETS):
            c = b + o - HALO
            if c < 0 or c >= nblocks:
                continue
            prod = lax.dot_general(
                x[:, c * width : (c + 1) * width],
                t_ref[b, o],
                (((1,), (1,)), ((), ())),
                preferred_element_type=jnp.float32,
            )
            acc = prod if acc is None else acc + prod
        o_ref[:, b * width : (b + 1) * width] = acc.astype(o_ref.dtype)


def column_pass(fields, terms, tile_rows=256):
    fields = fields if isinstance(fields, tuple) else (fields,)
    rows, cols = fields[0].shape
    tile = pl.BlockSpec((tile_rows, cols), lambda r: (r, 0))
    return pl.pallas_call(
        column_kernel,
        grid=(rows // tile_rows,),
        in_specs=[tile] * len(fields) + [pl.BlockSpec(terms.shape, lambda r: (0, 0, 0, 0))],
        out_specs=tile,
        out_shape=jax.ShapeDtypeStruct((rows, cols), jnp.bfloat16),
    )(*fields, terms)


def row_kernel(*refs, blocks, has_halo):
    if has_halo:
        prev_ref, mid_ref, next_ref, t_ref, o_ref = refs
    else:
        mid_ref, t_ref, o_ref = refs
    nlocal = t_ref.shape[0]
    width = t_ref.shape[2]
    for i, b in enumerate(blocks):
        acc = None
        for o in range(OFFSETS):
            e = b + o - HALO
            if e < 0:
                src = prev_ref[(e + HALO) * width : (e + HALO + 1) * width, :]
            elif e >= nlocal:
                src = next_ref[(e - nlocal) * width : (e - nlocal + 1) * width, :]
            else:
                src = mid_ref[e * width : (e + 1) * width, :]
            prod = jnp.dot(t_ref[b, o], src, preferred_element_type=jnp.float32)
            acc = prod if acc is None else acc + prod
        o_ref[i * width : (i + 1) * width, :] = acc.astype(o_ref.dtype)


def row_pass(mid, terms_local, blocks, halos=None, tile_cols=768):
    rows, cols = mid.shape
    width = terms_local.shape[2]
    tile = lambda r: pl.BlockSpec((r, tile_cols), lambda c: (0, c))
    operands = [mid, terms_local]
    specs = [tile(rows), pl.BlockSpec(terms_local.shape, lambda c: (0, 0, 0, 0))]
    if halos is not None:
        prev, nxt = halos
        operands = [prev, mid, nxt, terms_local]
        specs = [tile(prev.shape[0]), tile(rows), tile(nxt.shape[0]), specs[1]]
    return pl.pallas_call(
        functools.partial(row_kernel, blocks=tuple(blocks), has_halo=halos is not None),
        grid=(cols // tile_cols,),
        in_specs=specs,
        out_specs=tile(len(blocks) * width),
        out_shape=jax.ShapeDtypeStruct((len(blocks) * width, cols), jnp.bfloat16),
    )(*operands)


def per_device(image_masses, dual_multipliers, fraction_tops, banded_submatrices, band_starts, nslab):
    width = banded_submatrices.shape[2]
    rows = image_masses.shape[1]
    local_blocks = rows // width
    halo = HALO * width
    slab = lax.axis_index("slab")

    terms = offset_terms(banded_submatrices, band_starts)
    terms_local = lax.dynamic_slice_in_dim(terms, slab * local_blocks, local_blocks, axis=0)

    total_weight = lax.psum(jnp.sum(fraction_tops).astype(jnp.float32), "img")
    weight = fraction_tops.astype(jnp.float32)[0]

    up = [(i, i + 1) for i in range(nslab - 1)]
    down = [(i + 1, i) for i in range(nslab - 1)]

    def exchange(to_up, to_down):
        if nslab != 4:
            return lax.ppermute(to_up, "slab", up), lax.ppermute(to_down, "slab", down)
        half = halo // 2
        direct_prev = lax.ppermute(to_up, "slab", [(0, 1), (2, 3)])
        direct_next = lax.ppermute(to_down, "slab", [(1, 0), (3, 2)])
        first = jnp.where(slab == 1, to_up[:half], to_down[:half])
        second = jnp.where(slab == 1, to_up[half:], to_down[half:])
        first = lax.ppermute(first, "slab", [(1, 3), (2, 0)])
        second = lax.ppermute(second, "slab", [(1, 0), (2, 3)])
        first = lax.ppermute(first, "slab", [(3, 2), (0, 1)])
        second = lax.ppermute(second, "slab", [(0, 2), (3, 1)])
        diagonal = jnp.concatenate([first, second], axis=0)
        return jnp.where(slab == 2, diagonal, direct_prev), jnp.where(slab == 1, diagonal, direct_next)

    all_blocks = list(range(local_blocks))
    interior = all_blocks[HALO : local_blocks - HALO]
    boundary = all_blocks[:HALO] + all_blocks[local_blocks - HALO :] if interior else all_blocks

    def apply_kernel(field):
        inner = column_pass(field, terms)
        return row_pass(inner, terms_local, all_blocks, exchange(inner[rows - halo :], inner[:halo]))

    def apply_split(edges, inside):
        inner_edges = column_pass(edges, terms)
        halos = exchange(inner_edges[halo:], inner_edges[:halo])
        inner = jnp.concatenate([inner_edges[:halo], column_pass(inside, terms), inner_edges[halo:]], axis=0)
        return row_pass(inner, terms_local, all_blocks, halos)

    def log_sum(kernel_u):
        return lax.psum_scatter(weight * jnp.log(kernel_u), "img", scatter_dimension=0, tiled=True)

    def gather_barycenter(part_sum):
        return lax.all_gather(jnp.exp(part_sum / total_weight), "img", axis=0, tiled=True)

    def final_apply(field):
        inner = column_pass(field, terms)
        halos = exchange(inner[rows - halo :], inner[:halo])
        if not interior:
            kernel_u = row_pass(inner, terms_local, all_blocks, halos).astype(jnp.float32)
            return kernel_u, gather_barycenter(log_sum(kernel_u))
        inside = row_pass(inner, terms_local, interior).astype(jnp.float32)
        inside_sum = log_sum(inside)
        halos, inside_sum = lax.optimization_barrier((halos, inside_sum))
        edges = row_pass(inner, terms_local, boundary, halos).astype(jnp.float32)
        edges_bary = gather_barycenter(log_sum(edges))
        edges_bary, inside_sum = lax.optimization_barrier((edges_bary, inside_sum))
        inside_bary = gather_barycenter(inside_sum)
        return (edges, inside), (edges_bary, inside_bary)

    def assemble(parts):
        edges, inside = parts
        return jnp.concatenate([edges[:halo], inside, edges[halo:]], axis=0)

    def first_apply(field):
        halos = exchange(field[rows - halo :].astype(jnp.bfloat16), field[:halo].astype(jnp.bfloat16))
        inner = column_pass(field, terms)
        inner_halos = column_pass(jnp.concatenate(halos, axis=0), terms)
        return row_pass(inner, terms_local, all_blocks, (inner_halos[:halo], inner_halos[halo:]))

    masses = image_masses[0]
    scaling = dual_multipliers[0]
    kernel_v = first_apply(scaling)
    for iteration in range(ITERS):
        if iteration:
            if interior:
                side_edges, side_inside = [(b / k).astype(jnp.bfloat16) for b, k in zip(barycenter, kernel_u)]
                kernel_v = apply_split(side_edges, side_inside)
            else:
                kernel_v = apply_kernel((barycenter / kernel_u).astype(jnp.bfloat16))
        kernel_u, barycenter = final_apply((masses, kernel_v))
    if interior:
        kernel_u, barycenter = assemble(kernel_u), assemble(barycenter)
    return (barycenter, (barycenter / kernel_u)[None])


def solution(mesh):
    nslab = mesh.shape["slab"]
    placed = (P("img", "slab", None), P("img", "slab", None), P("img"), P(), P())

    def body(*args):
        return per_device(*args, nslab=nslab)

    return jax.shard_map(
        body,
        mesh=mesh,
        in_specs=placed,
        out_specs=(P("slab", None), P("img", "slab", None)),
        check_vma=False,
    )
```

```python
import functools

import jax
import jax.numpy as jnp
from jax import lax
from jax.experimental import pallas as pl
from jax.sharding import PartitionSpec as P

ITERS = 2
HALO = 2
OFFSETS = 2 * HALO + 1


def offset_terms(banded_submatrices, band_starts):
    offsets = jnp.arange(-HALO, HALO + 1, dtype=jnp.int32)
    matches = band_starts[:, None, :] == offsets[None, :, None]
    picked = jnp.where(matches[:, :, :, None, None], banded_submatrices[:, None], jnp.zeros((), jnp.bfloat16))
    return jnp.sum(picked, axis=2)


def column_kernel(*refs):
    *in_refs, t_ref, o_ref = refs
    nblocks = t_ref.shape[0]
    width = t_ref.shape[2]
    if len(in_refs) == 2:
        x = (in_refs[0][...] / in_refs[1][...].astype(jnp.float32)).astype(jnp.bfloat16)
    else:
        x = in_refs[0][...].astype(jnp.bfloat16)
    for b in range(nblocks):
        acc = None
        for o in range(OFFSETS):
            c = b + o - HALO
            if c < 0 or c >= nblocks:
                continue
            prod = lax.dot_general(
                x[:, c * width : (c + 1) * width],
                t_ref[b, o],
                (((1,), (1,)), ((), ())),
                preferred_element_type=jnp.float32,
            )
            acc = prod if acc is None else acc + prod
        o_ref[:, b * width : (b + 1) * width] = acc.astype(o_ref.dtype)


def column_pass(fields, terms, tile_rows=256):
    fields = fields if isinstance(fields, tuple) else (fields,)
    rows, cols = fields[0].shape
    tile = pl.BlockSpec((tile_rows, cols), lambda r: (r, 0))
    return pl.pallas_call(
        column_kernel,
        grid=(rows // tile_rows,),
        in_specs=[tile] * len(fields) + [pl.BlockSpec(terms.shape, lambda r: (0, 0, 0, 0))],
        out_specs=tile,
        out_shape=jax.ShapeDtypeStruct((rows, cols), jnp.bfloat16),
    )(*fields, terms)


def row_kernel(*refs, blocks, has_halo):
    if has_halo:
        prev_ref, mid_ref, next_ref, t_ref, o_ref = refs
    else:
        mid_ref, t_ref, o_ref = refs
    nlocal = t_ref.shape[0]
    width = t_ref.shape[2]
    for i, b in enumerate(blocks):
        acc = None
        for o in range(OFFSETS):
            e = b + o - HALO
            if e < 0:
                src = prev_ref[(e + HALO) * width : (e + HALO + 1) * width, :]
            elif e >= nlocal:
                src = next_ref[(e - nlocal) * width : (e - nlocal + 1) * width, :]
            else:
                src = mid_ref[e * width : (e + 1) * width, :]
            prod = jnp.dot(t_ref[b, o], src, preferred_element_type=jnp.float32)
            acc = prod if acc is None else acc + prod
        o_ref[i * width : (i + 1) * width, :] = acc.astype(o_ref.dtype)


def row_pass(mid, terms_local, blocks, halos=None, tile_cols=768):
    rows, cols = mid.shape
    width = terms_local.shape[2]
    tile = lambda r: pl.BlockSpec((r, tile_cols), lambda c: (0, c))
    operands = [mid, terms_local]
    specs = [tile(rows), pl.BlockSpec(terms_local.shape, lambda c: (0, 0, 0, 0))]
    if halos is not None:
        prev, nxt = halos
        operands = [prev, mid, nxt, terms_local]
        specs = [tile(prev.shape[0]), tile(rows), tile(nxt.shape[0]), specs[1]]
    return pl.pallas_call(
        functools.partial(row_kernel, blocks=tuple(blocks), has_halo=halos is not None),
        grid=(cols // tile_cols,),
        in_specs=specs,
        out_specs=tile(len(blocks) * width),
        out_shape=jax.ShapeDtypeStruct((len(blocks) * width, cols), jnp.bfloat16),
    )(*operands)


def per_device(image_masses, dual_multipliers, fraction_tops, banded_submatrices, band_starts, nslab):
    width = banded_submatrices.shape[2]
    rows = image_masses.shape[1]
    local_blocks = rows // width
    halo = HALO * width
    slab = lax.axis_index("slab")

    terms = offset_terms(banded_submatrices, band_starts)
    terms_local = lax.dynamic_slice_in_dim(terms, slab * local_blocks, local_blocks, axis=0)

    total_weight = lax.psum(jnp.sum(fraction_tops).astype(jnp.float32), "img")
    weight = fraction_tops.astype(jnp.float32)[0]

    up = [(i, i + 1) for i in range(nslab - 1)]
    down = [(i + 1, i) for i in range(nslab - 1)]

    def exchange(to_up, to_down):
        if nslab != 4:
            return lax.ppermute(to_up, "slab", up), lax.ppermute(to_down, "slab", down)
        half = halo // 2
        direct_prev = lax.ppermute(to_up, "slab", [(0, 1), (2, 3)])
        direct_next = lax.ppermute(to_down, "slab", [(1, 0), (3, 2)])
        first = jnp.where(slab == 1, to_up[:half], to_down[:half])
        second = jnp.where(slab == 1, to_up[half:], to_down[half:])
        first = lax.ppermute(first, "slab", [(1, 3), (2, 0)])
        second = lax.ppermute(second, "slab", [(1, 0), (2, 3)])
        first = lax.ppermute(first, "slab", [(3, 2), (0, 1)])
        second = lax.ppermute(second, "slab", [(0, 2), (3, 1)])
        diagonal = jnp.concatenate([first, second], axis=0)
        return jnp.where(slab == 2, diagonal, direct_prev), jnp.where(slab == 1, diagonal, direct_next)

    all_blocks = list(range(local_blocks))
    interior = all_blocks[HALO : local_blocks - HALO]
    boundary = all_blocks[:HALO] + all_blocks[local_blocks - HALO :] if interior else all_blocks

    def apply_kernel(field):
        inner = column_pass(field, terms)
        return row_pass(inner, terms_local, all_blocks, exchange(inner[rows - halo :], inner[:halo]))

    def apply_split(edges, inside):
        inner_edges = column_pass(edges, terms)
        halos = exchange(inner_edges[halo:], inner_edges[:halo])
        inner = jnp.concatenate([inner_edges[:halo], column_pass(inside, terms), inner_edges[halo:]], axis=0)
        return row_pass(inner, terms_local, all_blocks, halos)

    def log_sum(kernel_u):
        return lax.psum_scatter(weight * jnp.log(kernel_u), "img", scatter_dimension=0, tiled=True)

    def gather_barycenter(part_sum):
        return lax.all_gather(jnp.exp(part_sum / total_weight), "img", axis=0, tiled=True)

    def final_apply(field):
        inner = column_pass(field, terms)
        halos = exchange(inner[rows - halo :], inner[:halo])
        if not interior:
            kernel_u = row_pass(inner, terms_local, all_blocks, halos).astype(jnp.float32)
            return kernel_u, gather_barycenter(log_sum(kernel_u))
        inside = row_pass(inner, terms_local, interior).astype(jnp.float32)
        inside_sum = log_sum(inside)
        halos, inside_sum = lax.optimization_barrier((halos, inside_sum))
        edges = row_pass(inner, terms_local, boundary, halos).astype(jnp.float32)
        edges_bary = gather_barycenter(log_sum(edges))
        edges_bary, inside_sum = lax.optimization_barrier((edges_bary, inside_sum))
        inside_bary = gather_barycenter(inside_sum)
        return (edges, inside), (edges_bary, inside_bary)

    def assemble(parts):
        edges, inside = parts
        return jnp.concatenate([edges[:halo], inside, edges[halo:]], axis=0)

    masses = image_masses[0]
    scaling = dual_multipliers[0]
    kernel_v = apply_kernel(scaling)
    for iteration in range(ITERS):
        if iteration:
            if interior:
                kernel_v = apply_split(*zip(barycenter, kernel_u))
            else:
                kernel_v = apply_kernel((barycenter / kernel_u).astype(jnp.bfloat16))
        kernel_u, barycenter = final_apply((masses, kernel_v))
    if interior:
        kernel_u, barycenter = assemble(kernel_u), assemble(barycenter)
    return (barycenter, (barycenter / kernel_u)[None])


def solution(mesh):
    nslab = mesh.shape["slab"]
    placed = (P("img", "slab", None), P("img", "slab", None), P("img"), P(), P())

    def body(*args):
        return per_device(*args, nslab=nslab)

    return jax.shard_map(
        body,
        mesh=mesh,
        in_specs=placed,
        out_specs=(P("slab", None), P("img", "slab", None)),
        check_vma=False,
    )
```

```python
import functools

import jax
import jax.numpy as jnp
from jax import lax
from jax.experimental import pallas as pl
from jax.experimental.pallas import tpu as pltpu
from jax.sharding import PartitionSpec as P

ITERS = 2
HALO = 2
OFFSETS = 2 * HALO + 1


def offset_terms(banded_submatrices, band_starts):
    offsets = jnp.arange(-HALO, HALO + 1, dtype=jnp.int32)
    matches = band_starts[:, None, :] == offsets[None, :, None]
    picked = jnp.where(matches[:, :, :, None, None], banded_submatrices[:, None], jnp.zeros((), jnp.bfloat16))
    return jnp.sum(picked, axis=2)


def column_kernel(*refs):
    *in_refs, t_ref, o_ref = refs
    nblocks = t_ref.shape[0]
    width = t_ref.shape[2]
    if len(in_refs) == 2:
        x = (in_refs[0][...] / in_refs[1][...].astype(jnp.float32)).astype(jnp.bfloat16)
    else:
        x = in_refs[0][...].astype(jnp.bfloat16)
    for b in range(nblocks):
        acc = None
        for o in range(OFFSETS):
            c = b + o - HALO
            if c < 0 or c >= nblocks:
                continue
            prod = lax.dot_general(
                x[:, c * width : (c + 1) * width],
                t_ref[b, o],
                (((1,), (1,)), ((), ())),
                preferred_element_type=jnp.float32,
            )
            acc = prod if acc is None else acc + prod
        o_ref[:, b * width : (b + 1) * width] = acc.astype(o_ref.dtype)


def column_pass(fields, terms, tile_rows=256):
    fields = fields if isinstance(fields, tuple) else (fields,)
    rows, cols = fields[0].shape
    tile = pl.BlockSpec((tile_rows, cols), lambda r: (r, 0))
    return pl.pallas_call(
        column_kernel,
        grid=(rows // tile_rows,),
        in_specs=[tile] * len(fields) + [pl.BlockSpec(terms.shape, lambda r: (0, 0, 0, 0))],
        out_specs=tile,
        out_shape=jax.ShapeDtypeStruct((rows, cols), jnp.bfloat16),
    )(*fields, terms)


def row_kernel(*refs, blocks, has_halo, with_log):
    if with_log:
        *refs, w_ref, o_ref, log_ref = refs
    else:
        *refs, o_ref = refs
    if has_halo:
        prev_ref, mid_ref, next_ref, t_ref = refs
    else:
        mid_ref, t_ref = refs
    nlocal = t_ref.shape[0]
    width = t_ref.shape[2]
    for i, b in enumerate(blocks):
        acc = None
        for o in range(OFFSETS):
            e = b + o - HALO
            if e < 0:
                src = prev_ref[(e + HALO) * width : (e + HALO + 1) * width, :]
            elif e >= nlocal:
                src = next_ref[(e - nlocal) * width : (e - nlocal + 1) * width, :]
            else:
                src = mid_ref[e * width : (e + 1) * width, :]
            prod = jnp.dot(t_ref[b, o], src, preferred_element_type=jnp.float32)
            acc = prod if acc is None else acc + prod
        rounded = acc.astype(o_ref.dtype)
        o_ref[i * width : (i + 1) * width, :] = rounded
        if with_log:
            log_ref[i * width : (i + 1) * width, :] = w_ref[0] * jnp.log(rounded.astype(jnp.float32))


def row_pass(mid, terms_local, blocks, halos=None, weight=None, tile_cols=768):
    rows, cols = mid.shape
    width = terms_local.shape[2]
    tile = lambda r: pl.BlockSpec((r, tile_cols), lambda c: (0, c))
    operands = [mid, terms_local]
    specs = [tile(rows), pl.BlockSpec(terms_local.shape, lambda c: (0, 0, 0, 0))]
    if halos is not None:
        prev, nxt = halos
        operands = [prev, mid, nxt, terms_local]
        specs = [tile(prev.shape[0]), tile(rows), tile(nxt.shape[0]), specs[1]]
    out_rows = len(blocks) * width
    out_specs = tile(out_rows)
    out_shape = jax.ShapeDtypeStruct((out_rows, cols), jnp.bfloat16)
    if weight is not None:
        operands.append(weight.reshape((1,)))
        specs.append(pl.BlockSpec(memory_space=pltpu.SMEM))
        out_specs = [out_specs, tile(out_rows)]
        out_shape = [out_shape, jax.ShapeDtypeStruct((out_rows, cols), jnp.float32)]
    return pl.pallas_call(
        functools.partial(row_kernel, blocks=tuple(blocks), has_halo=halos is not None, with_log=weight is not None),
        grid=(cols // tile_cols,),
        in_specs=specs,
        out_specs=out_specs,
        out_shape=out_shape,
    )(*operands)


def per_device(image_masses, dual_multipliers, fraction_tops, banded_submatrices, band_starts, nslab):
    width = banded_submatrices.shape[2]
    rows = image_masses.shape[1]
    local_blocks = rows // width
    halo = HALO * width
    slab = lax.axis_index("slab")

    terms = offset_terms(banded_submatrices, band_starts)
    terms_local = lax.dynamic_slice_in_dim(terms, slab * local_blocks, local_blocks, axis=0)

    total_weight = lax.psum(jnp.sum(fraction_tops).astype(jnp.float32), "img")
    weight = fraction_tops.astype(jnp.float32)[0]

    up = [(i, i + 1) for i in range(nslab - 1)]
    down = [(i + 1, i) for i in range(nslab - 1)]

    def exchange(to_up, to_down):
        if nslab != 4:
            return lax.ppermute(to_up, "slab", up), lax.ppermute(to_down, "slab", down)
        half = halo // 2
        direct_prev = lax.ppermute(to_up, "slab", [(0, 1), (2, 3)])
        direct_next = lax.ppermute(to_down, "slab", [(1, 0), (3, 2)])
        first = jnp.where(slab == 1, to_up[:half], to_down[:half])
        second = jnp.where(slab == 1, to_up[half:], to_down[half:])
        first = lax.ppermute(first, "slab", [(1, 3), (2, 0)])
        second = lax.ppermute(second, "slab", [(1, 0), (2, 3)])
        first = lax.ppermute(first, "slab", [(3, 2), (0, 1)])
        second = lax.ppermute(second, "slab", [(0, 2), (3, 1)])
        diagonal = jnp.concatenate([first, second], axis=0)
        return jnp.where(slab == 2, diagonal, direct_prev), jnp.where(slab == 1, diagonal, direct_next)

    all_blocks = list(range(local_blocks))
    interior = all_blocks[HALO : local_blocks - HALO]
    boundary = all_blocks[:HALO] + all_blocks[local_blocks - HALO :] if interior else all_blocks

    def apply_kernel(field):
        inner = column_pass(field, terms)
        return row_pass(inner, terms_local, all_blocks, exchange(inner[rows - halo :], inner[:halo]))

    def apply_split(edges, inside):
        inner_edges = column_pass(edges, terms)
        halos = exchange(inner_edges[halo:], inner_edges[:halo])
        inner = jnp.concatenate([inner_edges[:halo], column_pass(inside, terms), inner_edges[halo:]], axis=0)
        return row_pass(inner, terms_local, all_blocks, halos)

    def log_sum(value_portion):
        return lax.psum_scatter(value_portion, "img", scatter_dimension=0, tiled=True)

    def gather_barycenter(part_sum):
        return lax.all_gather(jnp.exp(part_sum / total_weight), "img", axis=0, tiled=True)

    def final_apply(field):
        inner = column_pass(field, terms)
        halos = exchange(inner[rows - halo :], inner[:halo])
        if not interior:
            kernel_u, portion = row_pass(inner, terms_local, all_blocks, halos, weight)
            return kernel_u.astype(jnp.float32), gather_barycenter(log_sum(portion))
        inside, portion = row_pass(inner, terms_local, interior, weight=weight)
        inside = inside.astype(jnp.float32)
        inside_sum = log_sum(portion)
        halos, inside_sum = lax.optimization_barrier((halos, inside_sum))
        edges, portion = row_pass(inner, terms_local, boundary, halos, weight)
        edges = edges.astype(jnp.float32)
        edges_bary = gather_barycenter(log_sum(portion))
        edges_bary, inside_sum = lax.optimization_barrier((edges_bary, inside_sum))
        inside_bary = gather_barycenter(inside_sum)
        return (edges, inside), (edges_bary, inside_bary)

    def assemble(parts):
        edges, inside = parts
        return jnp.concatenate([edges[:halo], inside, edges[halo:]], axis=0)

    masses = image_masses[0]
    scaling = dual_multipliers[0]
    kernel_v = apply_kernel(scaling)
    for iteration in range(ITERS):
        if iteration:
            if interior:
                kernel_v = apply_split(*zip(barycenter, kernel_u))
            else:
                kernel_v = apply_kernel((barycenter / kernel_u).astype(jnp.bfloat16))
        kernel_u, barycenter = final_apply((masses, kernel_v))
    if interior:
        kernel_u, barycenter = assemble(kernel_u), assemble(barycenter)
    return (barycenter, (barycenter / kernel_u)[None])


def solution(mesh):
    nslab = mesh.shape["slab"]
    placed = (P("img", "slab", None), P("img", "slab", None), P("img"), P(), P())

    def body(*args):
        return per_device(*args, nslab=nslab)

    return jax.shard_map(
        body,
        mesh=mesh,
        in_specs=placed,
        out_specs=(P("slab", None), P("img", "slab", None)),
        check_vma=False,
    )
```

```python
import functools

import jax
import jax.numpy as jnp
from jax import lax
from jax.experimental import pallas as pl
from jax.experimental.pallas import tpu as pltpu
from jax.sharding import PartitionSpec as P

ITERS = 2
HALO = 2
OFFSETS = 2 * HALO + 1


def offset_terms(banded_submatrices, band_starts):
    offsets = jnp.arange(-HALO, HALO + 1, dtype=jnp.int32)
    matches = band_starts[:, None, :] == offsets[None, :, None]
    picked = jnp.where(matches[:, :, :, None, None], banded_submatrices[:, None], jnp.zeros((), jnp.bfloat16))
    return jnp.sum(picked, axis=2)


def column_kernel(*refs):
    *in_refs, t_ref, o_ref = refs
    nblocks = t_ref.shape[0]
    width = t_ref.shape[2]
    if len(in_refs) == 2:
        x = (in_refs[0][...] / in_refs[1][...].astype(jnp.float32)).astype(jnp.bfloat16)
    else:
        x = in_refs[0][...].astype(jnp.bfloat16)
    for b in range(nblocks):
        acc = None
        for o in range(OFFSETS):
            c = b + o - HALO
            if c < 0 or c >= nblocks:
                continue
            prod = lax.dot_general(
                x[:, c * width : (c + 1) * width],
                t_ref[b, o],
                (((1,), (1,)), ((), ())),
                preferred_element_type=jnp.float32,
            )
            acc = prod if acc is None else acc + prod
        o_ref[:, b * width : (b + 1) * width] = acc.astype(o_ref.dtype)


def column_pass(fields, terms, tile_rows=256):
    fields = fields if isinstance(fields, tuple) else (fields,)
    rows, cols = fields[0].shape
    tile = pl.BlockSpec((tile_rows, cols), lambda r: (r, 0))
    return pl.pallas_call(
        column_kernel,
        grid=(rows // tile_rows,),
        in_specs=[tile] * len(fields) + [pl.BlockSpec(terms.shape, lambda r: (0, 0, 0, 0))],
        out_specs=tile,
        out_shape=jax.ShapeDtypeStruct((rows, cols), jnp.bfloat16),
    )(*fields, terms)


def row_kernel(*refs, blocks, has_halo, with_log):
    if with_log:
        *refs, w_ref, o_ref, log_ref = refs
    else:
        *refs, o_ref = refs
    diag_ref = slab_ref = None
    if has_halo == 2:
        prev_ref, mid_ref, next_ref, t_ref, diag_ref, slab_ref = refs
    elif has_halo:
        prev_ref, mid_ref, next_ref, t_ref = refs
    else:
        mid_ref, t_ref = refs

    def halo_block(ref, start, owner):
        block = ref[start : start + width, :]
        if diag_ref is None:
            return block
        return jnp.where(slab_ref[0] == owner, diag_ref[start : start + width, :], block)

    nlocal = t_ref.shape[0]
    width = t_ref.shape[2]
    for i, b in enumerate(blocks):
        acc = None
        for o in range(OFFSETS):
            e = b + o - HALO
            if e < 0:
                src = halo_block(prev_ref, (e + HALO) * width, 2)
            elif e >= nlocal:
                src = halo_block(next_ref, (e - nlocal) * width, 1)
            else:
                src = mid_ref[e * width : (e + 1) * width, :]
            prod = jnp.dot(t_ref[b, o], src, preferred_element_type=jnp.float32)
            acc = prod if acc is None else acc + prod
        rounded = acc.astype(o_ref.dtype)
        o_ref[i * width : (i + 1) * width, :] = rounded
        if with_log:
            log_ref[i * width : (i + 1) * width, :] = w_ref[0] * jnp.log(rounded.astype(jnp.float32))


def row_pass(mid, terms_local, blocks, halos=None, weight=None, tile_cols=768):
    rows, cols = mid.shape
    width = terms_local.shape[2]
    tile = lambda r: pl.BlockSpec((r, tile_cols), lambda c: (0, c))
    operands = [mid, terms_local]
    specs = [tile(rows), pl.BlockSpec(terms_local.shape, lambda c: (0, 0, 0, 0))]
    has_halo = 0
    if halos is not None:
        prev, nxt, diagonal, slab_index = halos
        operands = [prev, mid, nxt, terms_local]
        specs = [tile(prev.shape[0]), tile(rows), tile(nxt.shape[0]), specs[1]]
        has_halo = 1
        if diagonal is not None:
            operands += [diagonal, slab_index]
            specs += [tile(diagonal.shape[0]), pl.BlockSpec(memory_space=pltpu.SMEM)]
            has_halo = 2
    out_rows = len(blocks) * width
    out_specs = tile(out_rows)
    out_shape = jax.ShapeDtypeStruct((out_rows, cols), jnp.bfloat16)
    if weight is not None:
        operands.append(weight.reshape((1,)))
        specs.append(pl.BlockSpec(memory_space=pltpu.SMEM))
        out_specs = [out_specs, tile(out_rows)]
        out_shape = [out_shape, jax.ShapeDtypeStruct((out_rows, cols), jnp.float32)]
    return pl.pallas_call(
        functools.partial(row_kernel, blocks=tuple(blocks), has_halo=has_halo, with_log=weight is not None),
        grid=(cols // tile_cols,),
        in_specs=specs,
        out_specs=out_specs,
        out_shape=out_shape,
    )(*operands)


def per_device(image_masses, dual_multipliers, fraction_tops, banded_submatrices, band_starts, nslab):
    width = banded_submatrices.shape[2]
    rows = image_masses.shape[1]
    local_blocks = rows // width
    halo = HALO * width
    slab = lax.axis_index("slab")

    terms = offset_terms(banded_submatrices, band_starts)
    terms_local = lax.dynamic_slice_in_dim(terms, slab * local_blocks, local_blocks, axis=0)

    total_weight = lax.psum(jnp.sum(fraction_tops).astype(jnp.float32), "img")
    weight = fraction_tops.astype(jnp.float32)[0]

    up = [(i, i + 1) for i in range(nslab - 1)]
    down = [(i + 1, i) for i in range(nslab - 1)]

    def exchange(to_up, to_down):
        if nslab != 4:
            return lax.ppermute(to_up, "slab", up), lax.ppermute(to_down, "slab", down), None, None
        half = halo // 2
        direct_prev = lax.ppermute(to_up, "slab", [(0, 1), (2, 3)])
        direct_next = lax.ppermute(to_down, "slab", [(1, 0), (3, 2)])
        first = jnp.where(slab == 1, to_up[:half], to_down[:half])
        second = jnp.where(slab == 1, to_up[half:], to_down[half:])
        first = lax.ppermute(first, "slab", [(1, 3), (2, 0)])
        second = lax.ppermute(second, "slab", [(1, 0), (2, 3)])
        first = lax.ppermute(first, "slab", [(3, 2), (0, 1)])
        second = lax.ppermute(second, "slab", [(0, 2), (3, 1)])
        diagonal = jnp.concatenate([first, second], axis=0)
        return direct_prev, direct_next, diagonal, slab.astype(jnp.int32).reshape((1,))

    all_blocks = list(range(local_blocks))
    interior = all_blocks[HALO : local_blocks - HALO]
    boundary = all_blocks[:HALO] + all_blocks[local_blocks - HALO :] if interior else all_blocks

    def apply_kernel(field):
        inner = column_pass(field, terms)
        return row_pass(inner, terms_local, all_blocks, exchange(inner[rows - halo :], inner[:halo]))

    def apply_split(edges, inside):
        inner_edges = column_pass(edges, terms)
        halos = exchange(inner_edges[halo:], inner_edges[:halo])
        inner = jnp.concatenate([inner_edges[:halo], column_pass(inside, terms), inner_edges[halo:]], axis=0)
        return row_pass(inner, terms_local, all_blocks, halos)

    def log_sum(value_portion):
        return lax.psum_scatter(value_portion, "img", scatter_dimension=0, tiled=True)

    def gather_barycenter(part_sum):
        return lax.all_gather(jnp.exp(part_sum / total_weight), "img", axis=0, tiled=True)

    def final_apply(field):
        inner = column_pass(field, terms)
        halos = exchange(inner[rows - halo :], inner[:halo])
        if not interior:
            kernel_u, portion = row_pass(inner, terms_local, all_blocks, halos, weight)
            return kernel_u.astype(jnp.float32), gather_barycenter(log_sum(portion))
        inside, portion = row_pass(inner, terms_local, interior, weight=weight)
        inside = inside.astype(jnp.float32)
        inside_sum = log_sum(portion)
        halos, inside_sum = lax.optimization_barrier((halos, inside_sum))
        edges, portion = row_pass(inner, terms_local, boundary, halos, weight)
        edges = edges.astype(jnp.float32)
        edges_bary = gather_barycenter(log_sum(portion))
        edges_bary, inside_sum = lax.optimization_barrier((edges_bary, inside_sum))
        inside_bary = gather_barycenter(inside_sum)
        return (edges, inside), (edges_bary, inside_bary)

    def assemble(parts):
        edges, inside = parts
        return jnp.concatenate([edges[:halo], inside, edges[halo:]], axis=0)

    masses = image_masses[0]
    scaling = dual_multipliers[0]
    kernel_v = apply_kernel(scaling)
    for iteration in range(ITERS):
        if iteration:
            if interior:
                kernel_v = apply_split(*zip(barycenter, kernel_u))
            else:
                kernel_v = apply_kernel((barycenter / kernel_u).astype(jnp.bfloat16))
        kernel_u, barycenter = final_apply((masses, kernel_v))
    if interior:
        kernel_u, barycenter = assemble(kernel_u), assemble(barycenter)
    return (barycenter, (barycenter / kernel_u)[None])


def solution(mesh):
    nslab = mesh.shape["slab"]
    placed = (P("img", "slab", None), P("img", "slab", None), P("img"), P(), P())

    def body(*args):
        return per_device(*args, nslab=nslab)

    return jax.shard_map(
        body,
        mesh=mesh,
        in_specs=placed,
        out_specs=(P("slab", None), P("img", "slab", None)),
        check_vma=False,
    )
```

```python
import functools

import jax
import jax.numpy as jnp
from jax import lax
from jax.experimental import pallas as pl
from jax.experimental.pallas import tpu as pltpu
from jax.sharding import PartitionSpec as P

ITERS = 2
HALO = 2
OFFSETS = 2 * HALO + 1


def offset_terms(banded_submatrices, band_starts):
    offsets = jnp.arange(-HALO, HALO + 1, dtype=jnp.int32)
    matches = band_starts[:, None, :] == offsets[None, :, None]
    picked = jnp.where(matches[:, :, :, None, None], banded_submatrices[:, None], jnp.zeros((), jnp.bfloat16))
    return jnp.sum(picked, axis=2)


def column_kernel(*refs):
    *in_refs, t_ref, o_ref = refs
    nblocks = t_ref.shape[0]
    width = t_ref.shape[2]
    if len(in_refs) == 2:
        x = (in_refs[0][...] / in_refs[1][...].astype(jnp.float32)).astype(jnp.bfloat16)
    else:
        x = in_refs[0][...].astype(jnp.bfloat16)
    for b in range(nblocks):
        acc = None
        for o in range(OFFSETS):
            c = b + o - HALO
            if c < 0 or c >= nblocks:
                continue
            prod = lax.dot_general(
                x[:, c * width : (c + 1) * width],
                t_ref[b, o],
                (((1,), (1,)), ((), ())),
                preferred_element_type=jnp.float32,
            )
            acc = prod if acc is None else acc + prod
        o_ref[:, b * width : (b + 1) * width] = acc.astype(o_ref.dtype)


def column_pass(fields, terms, tile_rows=256):
    fields = fields if isinstance(fields, tuple) else (fields,)
    rows, cols = fields[0].shape
    tile = pl.BlockSpec((tile_rows, cols), lambda r: (r, 0))
    return pl.pallas_call(
        column_kernel,
        grid=(rows // tile_rows,),
        in_specs=[tile] * len(fields) + [pl.BlockSpec(terms.shape, lambda r: (0, 0, 0, 0))],
        out_specs=tile,
        out_shape=jax.ShapeDtypeStruct((rows, cols), jnp.bfloat16),
    )(*fields, terms)


def row_kernel(*refs, blocks, has_halo, with_log):
    if with_log:
        *refs, w_ref, o_ref, log_ref = refs
    else:
        *refs, o_ref = refs
    if has_halo:
        prev_ref, mid_ref, next_ref, t_ref = refs
    else:
        mid_ref, t_ref = refs
    nlocal = t_ref.shape[0]
    width = t_ref.shape[2]
    for i, b in enumerate(blocks):
        acc = None
        for o in range(OFFSETS):
            e = b + o - HALO
            if e < 0:
                src = prev_ref[(e + HALO) * width : (e + HALO + 1) * width, :]
            elif e >= nlocal:
                src = next_ref[(e - nlocal) * width : (e - nlocal + 1) * width, :]
            else:
                src = mid_ref[e * width : (e + 1) * width, :]
            prod = jnp.dot(t_ref[b, o], src, preferred_element_type=jnp.float32)
            acc = prod if acc is None else acc + prod
        rounded = acc.astype(o_ref.dtype)
        o_ref[i * width : (i + 1) * width, :] = rounded
        if with_log:
            log_ref[i * width : (i + 1) * width, :] = w_ref[0] * jnp.log(rounded.astype(jnp.float32))


def row_pass(mid, terms_local, blocks, halos=None, weight=None, tile_cols=1536):
    rows, cols = mid.shape
    width = terms_local.shape[2]
    tile = lambda r: pl.BlockSpec((r, tile_cols), lambda c: (0, c))
    operands = [mid, terms_local]
    specs = [tile(rows), pl.BlockSpec(terms_local.shape, lambda c: (0, 0, 0, 0))]
    if halos is not None:
        prev, nxt = halos
        operands = [prev, mid, nxt, terms_local]
        specs = [tile(prev.shape[0]), tile(rows), tile(nxt.shape[0]), specs[1]]
    out_rows = len(blocks) * width
    out_specs = tile(out_rows)
    out_shape = jax.ShapeDtypeStruct((out_rows, cols), jnp.bfloat16)
    if weight is not None:
        operands.append(weight.reshape((1,)))
        specs.append(pl.BlockSpec(memory_space=pltpu.SMEM))
        out_specs = [out_specs, tile(out_rows)]
        out_shape = [out_shape, jax.ShapeDtypeStruct((out_rows, cols), jnp.float32)]
    return pl.pallas_call(
        functools.partial(row_kernel, blocks=tuple(blocks), has_halo=halos is not None, with_log=weight is not None),
        grid=(cols // tile_cols,),
        in_specs=specs,
        out_specs=out_specs,
        out_shape=out_shape,
    )(*operands)


def per_device(image_masses, dual_multipliers, fraction_tops, banded_submatrices, band_starts, nslab):
    width = banded_submatrices.shape[2]
    rows = image_masses.shape[1]
    local_blocks = rows // width
    halo = HALO * width
    slab = lax.axis_index("slab")

    terms = offset_terms(banded_submatrices, band_starts)
    terms_local = lax.dynamic_slice_in_dim(terms, slab * local_blocks, local_blocks, axis=0)

    total_weight = lax.psum(jnp.sum(fraction_tops).astype(jnp.float32), "img")
    weight = fraction_tops.astype(jnp.float32)[0]

    up = [(i, i + 1) for i in range(nslab - 1)]
    down = [(i + 1, i) for i in range(nslab - 1)]

    def exchange(to_up, to_down):
        if nslab != 4:
            return lax.ppermute(to_up, "slab", up), lax.ppermute(to_down, "slab", down)
        half = halo // 2
        direct_prev = lax.ppermute(to_up, "slab", [(0, 1), (2, 3)])
        direct_next = lax.ppermute(to_down, "slab", [(1, 0), (3, 2)])
        first = jnp.where(slab == 1, to_up[:half], to_down[:half])
        second = jnp.where(slab == 1, to_up[half:], to_down[half:])
        first = lax.ppermute(first, "slab", [(1, 3), (2, 0)])
        second = lax.ppermute(second, "slab", [(1, 0), (2, 3)])
        first = lax.ppermute(first, "slab", [(3, 2), (0, 1)])
        second = lax.ppermute(second, "slab", [(0, 2), (3, 1)])
        diagonal = jnp.concatenate([first, second], axis=0)
        return jnp.where(slab == 2, diagonal, direct_prev), jnp.where(slab == 1, diagonal, direct_next)

    all_blocks = list(range(local_blocks))
    interior = all_blocks[HALO : local_blocks - HALO]
    boundary = all_blocks[:HALO] + all_blocks[local_blocks - HALO :] if interior else all_blocks

    def apply_kernel(field):
        inner = column_pass(field, terms)
        return row_pass(inner, terms_local, all_blocks, exchange(inner[rows - halo :], inner[:halo]))

    def apply_split(edges, inside):
        inner_edges = column_pass(edges, terms)
        halos = exchange(inner_edges[halo:], inner_edges[:halo])
        inner = jnp.concatenate([inner_edges[:halo], column_pass(inside, terms), inner_edges[halo:]], axis=0)
        return row_pass(inner, terms_local, all_blocks, halos)

    def log_sum(value_portion):
        return lax.psum_scatter(value_portion, "img", scatter_dimension=0, tiled=True)

    def gather_barycenter(part_sum):
        return lax.all_gather(jnp.exp(part_sum / total_weight), "img", axis=0, tiled=True)

    def final_apply(field):
        inner = column_pass(field, terms)
        halos = exchange(inner[rows - halo :], inner[:halo])
        if not interior:
            kernel_u, portion = row_pass(inner, terms_local, all_blocks, halos, weight)
            return kernel_u.astype(jnp.float32), gather_barycenter(log_sum(portion))
        inside, portion = row_pass(inner, terms_local, interior, weight=weight)
        inside = inside.astype(jnp.float32)
        inside_sum = log_sum(portion)
        halos, inside_sum = lax.optimization_barrier((halos, inside_sum))
        edges, portion = row_pass(inner, terms_local, boundary, halos, weight)
        edges = edges.astype(jnp.float32)
        edges_bary = gather_barycenter(log_sum(portion))
        edges_bary, inside_sum = lax.optimization_barrier((edges_bary, inside_sum))
        inside_bary = gather_barycenter(inside_sum)
        return (edges, inside), (edges_bary, inside_bary)

    def assemble(parts):
        edges, inside = parts
        return jnp.concatenate([edges[:halo], inside, edges[halo:]], axis=0)

    masses = image_masses[0]
    scaling = dual_multipliers[0]
    kernel_v = apply_kernel(scaling)
    for iteration in range(ITERS):
        if iteration:
            if interior:
                kernel_v = apply_split(*zip(barycenter, kernel_u))
            else:
                kernel_v = apply_kernel((barycenter / kernel_u).astype(jnp.bfloat16))
        kernel_u, barycenter = final_apply((masses, kernel_v))
    if interior:
        kernel_u, barycenter = assemble(kernel_u), assemble(barycenter)
    return (barycenter, (barycenter / kernel_u)[None])


def solution(mesh):
    nslab = mesh.shape["slab"]
    placed = (P("img", "slab", None), P("img", "slab", None), P("img"), P(), P())

    def body(*args):
        return per_device(*args, nslab=nslab)

    return jax.shard_map(
        body,
        mesh=mesh,
        in_specs=placed,
        out_specs=(P("slab", None), P("img", "slab", None)),
        check_vma=False,
    )
```

```python
import functools

import jax
import jax.numpy as jnp
from jax import lax
from jax.experimental import pallas as pl
from jax.experimental.pallas import tpu as pltpu
from jax.sharding import PartitionSpec as P

ITERS = 2
HALO = 2
OFFSETS = 2 * HALO + 1


def offset_terms(banded_submatrices, band_starts):
    offsets = jnp.arange(-HALO, HALO + 1, dtype=jnp.int32)
    matches = band_starts[:, None, :] == offsets[None, :, None]
    picked = jnp.where(matches[:, :, :, None, None], banded_submatrices[:, None], jnp.zeros((), jnp.bfloat16))
    return jnp.sum(picked, axis=2)


def column_kernel(*refs):
    *in_refs, t_ref, o_ref = refs
    nblocks = t_ref.shape[0]
    width = t_ref.shape[2]
    if len(in_refs) == 2:
        x = (in_refs[0][...] / in_refs[1][...].astype(jnp.float32)).astype(jnp.bfloat16)
    else:
        x = in_refs[0][...].astype(jnp.bfloat16)
    for b in range(nblocks):
        acc = None
        for o in range(OFFSETS):
            c = b + o - HALO
            if c < 0 or c >= nblocks:
                continue
            prod = lax.dot_general(
                x[:, c * width : (c + 1) * width],
                t_ref[b, o],
                (((1,), (1,)), ((), ())),
                preferred_element_type=jnp.float32,
            )
            acc = prod if acc is None else acc + prod
        o_ref[:, b * width : (b + 1) * width] = acc.astype(o_ref.dtype)


def column_pass(fields, terms, tile_rows=384):
    fields = fields if isinstance(fields, tuple) else (fields,)
    rows, cols = fields[0].shape
    if rows % tile_rows:
        tile_rows = 256
    tile = pl.BlockSpec((tile_rows, cols), lambda r: (r, 0))
    return pl.pallas_call(
        column_kernel,
        grid=(rows // tile_rows,),
        in_specs=[tile] * len(fields) + [pl.BlockSpec(terms.shape, lambda r: (0, 0, 0, 0))],
        out_specs=tile,
        out_shape=jax.ShapeDtypeStruct((rows, cols), jnp.bfloat16),
    )(*fields, terms)


def row_kernel(*refs, blocks, has_halo, with_log):
    if with_log:
        *refs, w_ref, o_ref, log_ref = refs
    else:
        *refs, o_ref = refs
    if has_halo:
        prev_ref, mid_ref, next_ref, t_ref = refs
    else:
        mid_ref, t_ref = refs
    nlocal = t_ref.shape[0]
    width = t_ref.shape[2]
    for i, b in enumerate(blocks):
        acc = None
        for o in range(OFFSETS):
            e = b + o - HALO
            if e < 0:
                src = prev_ref[(e + HALO) * width : (e + HALO + 1) * width, :]
            elif e >= nlocal:
                src = next_ref[(e - nlocal) * width : (e - nlocal + 1) * width, :]
            else:
                src = mid_ref[e * width : (e + 1) * width, :]
            prod = jnp.dot(t_ref[b, o], src, preferred_element_type=jnp.float32)
            acc = prod if acc is None else acc + prod
        rounded = acc.astype(o_ref.dtype)
        o_ref[i * width : (i + 1) * width, :] = rounded
        if with_log:
            log_ref[i * width : (i + 1) * width, :] = w_ref[0] * jnp.log(rounded.astype(jnp.float32))


def row_pass(mid, terms_local, blocks, halos=None, weight=None, tile_cols=1536):
    rows, cols = mid.shape
    width = terms_local.shape[2]
    tile = lambda r: pl.BlockSpec((r, tile_cols), lambda c: (0, c))
    operands = [mid, terms_local]
    specs = [tile(rows), pl.BlockSpec(terms_local.shape, lambda c: (0, 0, 0, 0))]
    if halos is not None:
        prev, nxt = halos
        operands = [prev, mid, nxt, terms_local]
        specs = [tile(prev.shape[0]), tile(rows), tile(nxt.shape[0]), specs[1]]
    out_rows = len(blocks) * width
    out_specs = tile(out_rows)
    out_shape = jax.ShapeDtypeStruct((out_rows, cols), jnp.bfloat16)
    if weight is not None:
        operands.append(weight.reshape((1,)))
        specs.append(pl.BlockSpec(memory_space=pltpu.SMEM))
        out_specs = [out_specs, tile(out_rows)]
        out_shape = [out_shape, jax.ShapeDtypeStruct((out_rows, cols), jnp.float32)]
    return pl.pallas_call(
        functools.partial(row_kernel, blocks=tuple(blocks), has_halo=halos is not None, with_log=weight is not None),
        grid=(cols // tile_cols,),
        in_specs=specs,
        out_specs=out_specs,
        out_shape=out_shape,
    )(*operands)


def per_device(image_masses, dual_multipliers, fraction_tops, banded_submatrices, band_starts, nslab):
    width = banded_submatrices.shape[2]
    rows = image_masses.shape[1]
    local_blocks = rows // width
    halo = HALO * width
    slab = lax.axis_index("slab")

    terms = offset_terms(banded_submatrices, band_starts)
    terms_local = lax.dynamic_slice_in_dim(terms, slab * local_blocks, local_blocks, axis=0)

    total_weight = lax.psum(jnp.sum(fraction_tops).astype(jnp.float32), "img")
    weight = fraction_tops.astype(jnp.float32)[0]

    up = [(i, i + 1) for i in range(nslab - 1)]
    down = [(i + 1, i) for i in range(nslab - 1)]

    def exchange(to_up, to_down):
        if nslab != 4:
            return lax.ppermute(to_up, "slab", up), lax.ppermute(to_down, "slab", down)
        half = halo // 2
        direct_prev = lax.ppermute(to_up, "slab", [(0, 1), (2, 3)])
        direct_next = lax.ppermute(to_down, "slab", [(1, 0), (3, 2)])
        first = jnp.where(slab == 1, to_up[:half], to_down[:half])
        second = jnp.where(slab == 1, to_up[half:], to_down[half:])
        first = lax.ppermute(first, "slab", [(1, 3), (2, 0)])
        second = lax.ppermute(second, "slab", [(1, 0), (2, 3)])
        first = lax.ppermute(first, "slab", [(3, 2), (0, 1)])
        second = lax.ppermute(second, "slab", [(0, 2), (3, 1)])
        diagonal = jnp.concatenate([first, second], axis=0)
        return jnp.where(slab == 2, diagonal, direct_prev), jnp.where(slab == 1, diagonal, direct_next)

    all_blocks = list(range(local_blocks))
    interior = all_blocks[HALO : local_blocks - HALO]
    boundary = all_blocks[:HALO] + all_blocks[local_blocks - HALO :] if interior else all_blocks

    def apply_kernel(field):
        inner = column_pass(field, terms)
        return row_pass(inner, terms_local, all_blocks, exchange(inner[rows - halo :], inner[:halo]))

    def apply_split(edges, inside):
        inner_edges = column_pass(edges, terms)
        halos = exchange(inner_edges[halo:], inner_edges[:halo])
        inner = jnp.concatenate([inner_edges[:halo], column_pass(inside, terms), inner_edges[halo:]], axis=0)
        return row_pass(inner, terms_local, all_blocks, halos)

    def log_sum(value_portion):
        return lax.psum_scatter(value_portion, "img", scatter_dimension=0, tiled=True)

    def gather_barycenter(part_sum):
        return lax.all_gather(jnp.exp(part_sum / total_weight), "img", axis=0, tiled=True)

    def final_apply(field):
        inner = column_pass(field, terms)
        halos = exchange(inner[rows - halo :], inner[:halo])
        if not interior:
            kernel_u, portion = row_pass(inner, terms_local, all_blocks, halos, weight)
            return kernel_u.astype(jnp.float32), gather_barycenter(log_sum(portion))
        inside, portion = row_pass(inner, terms_local, interior, weight=weight)
        inside = inside.astype(jnp.float32)
        inside_sum = log_sum(portion)
        halos, inside_sum = lax.optimization_barrier((halos, inside_sum))
        edges, portion = row_pass(inner, terms_local, boundary, halos, weight)
        edges = edges.astype(jnp.float32)
        edges_bary = gather_barycenter(log_sum(portion))
        edges_bary, inside_sum = lax.optimization_barrier((edges_bary, inside_sum))
        inside_bary = gather_barycenter(inside_sum)
        return (edges, inside), (edges_bary, inside_bary)

    def assemble(parts):
        edges, inside = parts
        return jnp.concatenate([edges[:halo], inside, edges[halo:]], axis=0)

    masses = image_masses[0]
    scaling = dual_multipliers[0]
    kernel_v = apply_kernel(scaling)
    for iteration in range(ITERS):
        if iteration:
            if interior:
                kernel_v = apply_split(*zip(barycenter, kernel_u))
            else:
                kernel_v = apply_kernel((barycenter / kernel_u).astype(jnp.bfloat16))
        kernel_u, barycenter = final_apply((masses, kernel_v))
    if interior:
        kernel_u, barycenter = assemble(kernel_u), assemble(barycenter)
    return (barycenter, (barycenter / kernel_u)[None])


def solution(mesh):
    nslab = mesh.shape["slab"]
    placed = (P("img", "slab", None), P("img", "slab", None), P("img"), P(), P())

    def body(*args):
        return per_device(*args, nslab=nslab)

    return jax.shard_map(
        body,
        mesh=mesh,
        in_specs=placed,
        out_specs=(P("slab", None), P("img", "slab", None)),
        check_vma=False,
    )
```
